512 devices in a mesh: section: 4 (over z_hi, core), seq: 32 (over x, y), head: 4 (over z_lo).
Axes of the slice: x: 4, y: 8, z: 8 (z_hi: 2, z_lo: 4; z = z_hi * 4 + z_lo), core: 2. Of those that a mesh axis runs over, the one named last changes fastest.
Arguments:
- query_heads: bfloat16 [4, 6144, 3072], P('section', 'seq', 'head'), may hold values from -6 to 6
- key_heads: bfloat16 [4, 6144, 3072], P('section', 'seq', 'head'), may hold values from -6 to 6
- value_heads: bfloat16 [4, 6144, 3072], P('section', 'seq', 'head'), may hold values from -6 to 6
- stream: bfloat16 [4, 6144, 3072], P('section', 'seq', 'head'), may hold values from -1.5 to 1.5
- out_weight: bfloat16 [4, 3072, 3072], P('section', 'head', 'seq'), may hold values from -0.109375 to 0.109375
- gate_scale: float32 [4, 3072], P('section', 'head'), may hold values from 0.5 to 1.5
- windows: int32 [16, 27], replicated, may hold values from -1 to 15, as said below
Outputs:
- handed: bfloat16 [4, 6144, 3072], P('section', 'seq', 'head')
The draws below stay inside these ranges and needn't reach their ends.
Inputs may be any that keep to these rules, and one draw needn't show every extreme that they name: `windows`: row t lists, in an order drawn for each row, tile t + dt for every dt in -1, 0, 1 with 0 <= t + dt < 16 and tile t + dt in the same clip as t, and -1 in all its other slots; clips are runs of whole consecutive temporal tiles.
All inputs are finite; a program needn't handle non-finite values.
Results may differ from the reference program's by a relative error of at most 0.012.
Values may be sent and summed in bfloat16 or wider, within the bound.
No kernel may reach another device: no remote copies, remote signals or barrier semaphores. Data moves between devices by JAX's collectives and lax.ppermute only.
A program may use at most 64 MiB of HBM per device.

```python
import math
import jax
import jax.numpy as jnp
from jax import lax

D = 3072
HEADS = 24
HD = 128
SPATIAL = 1
TOKENS = 6144
TILES = 16
SECTIONS = 4
N_HEAD = 4


def drawn_values(key, salt, normal_scale):
    return jnp.clip(normal_scale * jax.random.normal(jax.random.fold_in(key, salt), (SECTIONS, TOKENS, HEADS * HD), jnp.float32), -6.0, 6.0)


def draw_query_heads(key, part):
    drawn_draw = drawn_values(key, 21, 4.0)
    return drawn_draw.astype(jnp.bfloat16)


def draw_key_heads(key, part):
    drawn_draw = drawn_values(key, 22, 0.9)
    return drawn_draw.astype(jnp.bfloat16)


def row_order(key, row_index):
    return jax.random.permutation(jax.random.fold_in(key, row_index), 27)


def draw_windows(key, part):
    temporal_count = TILES // SPATIAL
    cut_draw = jax.random.randint(jax.random.fold_in(key, 31), (temporal_count,), 0, 3)
    clip_starts = jnp.where(jnp.arange(temporal_count) == 0, 1, (cut_draw == 0).astype(jnp.int32))
    clip_ids = jnp.cumsum(clip_starts)
    slots = jnp.arange(27)
    delta_time = slots // 9 - 1
    delta_height = slots // 3 % 3 - 1
    delta_width = slots % 3 - 1
    times = jnp.arange(temporal_count)[:, None, None]
    places = jnp.arange(SPATIAL)[None, :, None]
    near_time = times + delta_time[None, None, :]
    near_place = places + delta_width[None, None, :]
    inside = (near_time >= 0) & (near_time < temporal_count) & (delta_height[None, None, :] == 0)
    inside = inside & (near_place >= 0) & (near_place < SPATIAL)
    same_clip = clip_ids[jnp.clip(near_time, 0, temporal_count - 1)] == clip_ids[times]
    tile_ids = jnp.where(inside & same_clip, near_time * SPATIAL + near_place, -1).reshape(TILES, 27)
    order_key = jax.random.fold_in(key, 41)
    orders = jax.vmap(lambda row_index: row_order(order_key, row_index))(jnp.arange(TILES))
    return jnp.take_along_axis(tile_ids, orders, axis=1).astype(jnp.int32)


def steps_of(key, extent, split, smallest, largest):
    def one(position, blocks):
        heights = jax.random.uniform(jax.random.fold_in(jax.random.fold_in(key, 6), position), (blocks,), jnp.float32, smallest / len(split), largest / len(split))
        return jnp.repeat(jnp.exp(heights), extent[position] // blocks).reshape((-1,) + (1,) * (len(extent) - position - 1))

    factor_of = one(*split[0])
    for cut in split[1:]:
        factor_of = factor_of * one(*cut)
    return factor_of


def bell_draw(rng, extent, spread, reach, split=(), kind=jnp.bfloat16):
    gain = steps_of(rng, extent, split, -0.22, 0.18) if split else 1.0
    drawn = jax.random.normal(rng, extent, jnp.float32) * spread * gain
    return jnp.minimum(jnp.maximum(drawn, -reach), reach).astype(kind)


def setup_inputs(seed: int = 0) -> dict:
    seeds = jax.random.split(jax.random.key(seed), 8)
    query_heads = draw_query_heads(jax.random.fold_in(seeds[7], 71), 0)
    key_heads = draw_key_heads(jax.random.fold_in(seeds[7], 71), 0)
    value_heads = bell_draw(seeds[2], (SECTIONS, TOKENS, HEADS * HD), 1.0, 6.0, ((0, 4), (1, 32), (2, 4)))
    stream = bell_draw(seeds[3], (SECTIONS, TOKENS, D), 0.1, 1.5, ((0, 4), (1, 32), (2, 4)))
    out_weight = bell_draw(seeds[4], (SECTIONS, HEADS * HD, D), (HEADS * HD) ** -0.5, 0.109375, ((0, 4), (1, 4), (2, 32)))
    gate_scale = jnp.clip(0.5 + 1.0 * jax.random.uniform(seeds[5], (SECTIONS, D), jnp.float32) ** steps_of(seeds[5], (SECTIONS, D), ((0, 4), (1, 4)), -0.2, 0.2), 0.5, 1.5)
    windows = draw_windows(jax.random.fold_in(seeds[7], 71), 0)
    return dict(query_heads=query_heads, key_heads=key_heads, value_heads=value_heads, stream=stream, out_weight=out_weight, gate_scale=gate_scale, windows=windows)


def tile_layout(array, temporal_count):
    feature_count = array.shape[-1]
    half_rows = array.shape[0] // (2 * temporal_count * SPATIAL)
    shaped = array.reshape(temporal_count, 2, SPATIAL, half_rows, feature_count).transpose(0, 2, 1, 3, 4)
    return shaped.reshape(temporal_count, SPATIAL, 2 * half_rows, feature_count)

def token_layout(array, temporal_count):
    feature_count = array.shape[-1]
    half_rows = array.shape[2] // 2
    shaped = array.reshape(temporal_count, SPATIAL, 2, half_rows, feature_count).transpose(0, 2, 1, 3, 4)
    return shaped.reshape(-1, feature_count)

def attend_section(queries, keys_all, values_all, allowed):
    temporal_count = allowed.shape[0] // SPATIAL
    score_scale = 1.0 / math.sqrt(HD)
    q_tiles = tile_layout(queries, temporal_count)
    tile_len = q_tiles.shape[2]
    q_tiles = q_tiles.reshape(temporal_count, SPATIAL, tile_len, HEADS, HD)
    k_tiles = tile_layout(keys_all, temporal_count).reshape(temporal_count, SPATIAL, tile_len, HEADS, HD)
    v_tiles = tile_layout(values_all, temporal_count).reshape(temporal_count, SPATIAL, tile_len, HEADS, HD)
    k_pad = jnp.pad(k_tiles, ((1, 1), (0, 0), (0, 0), (0, 0), (0, 0)))
    v_pad = jnp.pad(v_tiles, ((1, 1), (0, 0), (0, 0), (0, 0), (0, 0)))
    k_float = k_pad.astype(jnp.float32)
    tile_max = lax.optimization_barrier(jnp.max(jnp.sqrt(lax.optimization_barrier(jnp.sum(k_float * k_float, axis=-1))), axis=2))

    def one_tile(tile_index):
        query_tile = lax.dynamic_index_in_dim(q_tiles, tile_index, 0, keepdims=False)
        key_tile = lax.dynamic_slice_in_dim(k_pad, tile_index, 3, 0)
        value_tile = lax.dynamic_slice_in_dim(v_pad, tile_index, 3, 0)
        max_tile = lax.dynamic_slice_in_dim(tile_max, tile_index, 3, 0)
        times = tile_index - 1 + jnp.arange(3, dtype=jnp.int32)
        in_range = (times >= 0) & (times < temporal_count)
        tile_ids = jnp.clip(times, 0, temporal_count - 1)[:, None] * SPATIAL + jnp.arange(SPATIAL, dtype=jnp.int32)[None, :]
        row_allowed = lax.dynamic_slice_in_dim(allowed, (tile_index * SPATIAL).astype(jnp.int32), SPATIAL, 0)
        keep = jnp.take(row_allowed, tile_ids.reshape(-1), axis=1).reshape(SPATIAL, 3, SPATIAL) & in_range[None, :, None]
        bound_tile = lax.optimization_barrier(jnp.max(jnp.where(keep[:, :, :, None], max_tile[None], 0.0), axis=(1, 2)))
        query_float = query_tile.astype(jnp.float32)
        query_len = jnp.sqrt(lax.optimization_barrier(jnp.sum(query_float * query_float, axis=-1)))
        row_bound = (query_len * bound_tile[:, None, :] * score_scale).reshape(SPATIAL * tile_len, HEADS)
        query_flat = query_float.reshape(SPATIAL * tile_len, HEADS, HD)
        key_flat = key_tile.astype(jnp.float32).reshape(3 * SPATIAL * tile_len, HEADS, HD)
        value_flat = value_tile.astype(jnp.float32).reshape(3 * SPATIAL * tile_len, HEADS, HD)
        scores = jnp.einsum('qhd,khd->hqk', query_flat, key_flat) * score_scale
        row_keep = jnp.broadcast_to(keep[:, None, :, :, None], (SPATIAL, tile_len, 3, SPATIAL, tile_len))
        row_keep = row_keep.reshape(SPATIAL * tile_len, 3 * SPATIAL * tile_len)
        weights = jnp.where(row_keep[None], jnp.exp(scores - row_bound.T[:, :, None]), 0.0)
        summed = lax.optimization_barrier(jnp.sum(weights, axis=2))
        rounded = weights.astype(jnp.bfloat16).astype(jnp.float32)
        weighted = jnp.einsum('hqk,khd->qhd', rounded, value_flat)
        attended = (weighted / summed.T[:, :, None]).astype(jnp.bfloat16)
        return attended.reshape(SPATIAL, tile_len, HEADS * HD)
    tiles_out = lax.map(one_tile, jnp.arange(temporal_count, dtype=jnp.int32))
    return token_layout(tiles_out, temporal_count)

def reference(query_heads, key_heads, value_heads, stream, out_weight, gate_scale, windows):
    tile_count = windows.shape[0]
    allowed = jnp.any(windows[:, :, None] == jnp.arange(tile_count, dtype=jnp.int32)[None, None, :], axis=1)
    group_width = HEADS * HD // N_HEAD

    def one_section(inputs):
        queries, keys_all, values_all, section_stream, weight, section_gate = inputs
        attended = attend_section(queries, keys_all, values_all, allowed)
        mixed = jnp.zeros((attended.shape[0], D), jnp.float32)
        for head_group in range(N_HEAD):
            term = jnp.dot(attended[:, head_group * group_width:(head_group + 1) * group_width], weight[head_group * group_width:(head_group + 1) * group_width], preferred_element_type=jnp.float32)
            mixed = mixed + lax.optimization_barrier(term.astype(jnp.bfloat16)).astype(jnp.float32)
        return (section_stream.astype(jnp.float32) + section_gate[None, :] * mixed).astype(jnp.bfloat16)
    updated = lax.map(one_section, (query_heads, key_heads, value_heads, stream, out_weight, gate_scale))
    return jnp.roll(updated, 1, axis=0)
```

```python
from functools import partial
import math

import jax
import jax.numpy as jnp
from jax import lax
from jax.sharding import Mesh, PartitionSpec as P

HD = 128
SPATIAL = 1


def shifted(block, axis, count, distance, wanted):
    devices = range(count)
    route = [(i - distance, i) for i in devices if i - distance in devices and wanted(i)]
    return lax.ppermute(block, axis, route)


def needs(offset):
    if offset == 3:
        return lambda i: i % 2 == 1
    if offset == -3:
        return lambda i: i % 2 == 0
    return lambda i: True


def linear_pairs(sizes, mapping):
    def flat(index):
        value = 0
        for part, size in zip(index, sizes):
            value = value * size + part
        return value

    grid = [[]]
    for size in sizes:
        grid = [index + [part] for index in grid for part in range(size)]
    return [(flat(index), flat(mapping(*index))) for index in grid]


def from_behind(value, axis, steps):
    count = lax.axis_size(axis)
    pairs = [(source, (source + steps) % count) for source in range(count)]
    return lax.ppermute(value, axis, pairs)


def split_heads(slab, head_count):
    return slab.reshape(slab.shape[0], head_count, slab.shape[1] // head_count)


def tile_maxima(key_slab, head_count, spatial_count):
    parts = split_heads(key_slab, head_count).astype(jnp.float32)
    lengths = jnp.sqrt(jnp.sum(parts * parts, axis=2))
    return jnp.max(lengths.reshape(spatial_count, -1, head_count), axis=1)


def slab_keep(nearby, slab_tile, in_range, spatial_count, temporal_count):
    first = jnp.clip(slab_tile, 0, temporal_count - 1) * spatial_count
    return lax.dynamic_slice_in_dim(nearby, first, spatial_count, 1) & in_range


def attend(
    running,
    slab_entry,
    keep,
    query_parts,
    row_bound,
    head_count,
    spatial_count,
    tile_rows,
    score_scale,
):
    weighted, summed = running
    row_count = query_parts.shape[0]
    slab_keys = split_heads(slab_entry[0], head_count)
    slab_values = split_heads(slab_entry[1], head_count)
    scores = (
        jnp.einsum("qhd,khd->hqk", query_parts, slab_keys, preferred_element_type=jnp.float32)
        * score_scale
    )
    row_keep = jnp.broadcast_to(
        keep[:, None, :, None], (spatial_count, tile_rows, spatial_count, tile_rows)
    )
    row_keep = row_keep.reshape(row_count, row_count)
    weights = jnp.where(row_keep[None], jnp.exp(scores - row_bound.T[:, :, None]), 0.0)
    summed = summed + jnp.sum(weights, axis=2)
    weighted = weighted + jnp.einsum(
        "hqk,khd->qhd",
        weights.astype(jnp.bfloat16),
        slab_values,
        preferred_element_type=jnp.float32,
    )
    return (weighted, summed)


def on_device(query_heads, key_heads, value_heads, stream, out_weight, gate_scale, windows):
    queries = query_heads[0]
    own_keys = key_heads[0]
    own_values = value_heads[0]
    row_count, feature_count = queries.shape
    head_count = feature_count // HD
    spatial_count = SPATIAL
    tile_rows = row_count // spatial_count
    tile_count = windows.shape[0]
    temporal_count = tile_count // spatial_count
    score_scale = 1.0 / math.sqrt(HD)
    x_count = lax.axis_size("sx")
    y_count = lax.axis_size("sy")
    head_groups = lax.axis_size("head")
    sections = lax.axis_size("section")
    seq_count = x_count * y_count
    x_index = lax.axis_index("sx")
    y_index = lax.axis_index("sy")
    position = x_index * y_count + y_index
    temporal = position // 2
    allowed = jnp.any(
        windows[:, :, None] == jnp.arange(tile_count, dtype=jnp.int32)[None, None, :], axis=1
    )
    nearby = lax.dynamic_slice_in_dim(allowed, temporal * spatial_count, spatial_count, 0)
    always = jnp.array(True)
    slabs = [(own_keys, own_values, temporal, always)]
    reach = min(3, seq_count - 1)
    offsets = list(range(1, reach + 1)) + list(range(-reach, 0))
    for offset in offsets:
        moved_keys, moved_values = shifted(
            (own_keys, own_values), ("sx", "sy"), seq_count, offset, needs(offset)
        )
        source = position - offset
        in_range = (source >= 0) & (source < seq_count)
        slabs.append((moved_keys, moved_values, source // 2, in_range))
    keeps = [
        slab_keep(nearby, slab_entry[2], slab_entry[3], spatial_count, temporal_count)
        for slab_entry in slabs
    ]
    bound_tiles = jnp.zeros((spatial_count, head_count), jnp.float32)
    for slab_entry, keep in zip(slabs, keeps):
        maxima = tile_maxima(slab_entry[0], head_count, spatial_count)
        candidate = jnp.where(keep[:, :, None], maxima[None, :, :], 0.0)
        bound_tiles = jnp.maximum(bound_tiles, jnp.max(candidate, axis=1))
    query_parts = split_heads(queries, head_count)
    query_float = query_parts.astype(jnp.float32)
    query_lengths = jnp.sqrt(jnp.sum(query_float * query_float, axis=2))
    row_bound = query_lengths * jnp.repeat(bound_tiles, tile_rows, axis=0) * score_scale
    running = (
        jnp.zeros((row_count, head_count, HD), jnp.float32),
        jnp.zeros((head_count, row_count), jnp.float32),
    )
    for slab_entry, keep in zip(slabs, keeps):
        step_fn = partial(
            attend,
            slab_entry=slab_entry,
            keep=keep,
            query_parts=query_parts,
            row_bound=row_bound,
            head_count=head_count,
            spatial_count=spatial_count,
            tile_rows=tile_rows,
            score_scale=score_scale,
        )
        running = step_fn(running)
    weighted, summed = running
    attended = (
        (weighted / summed.T[:, :, None]).astype(jnp.bfloat16).reshape(row_count, feature_count)
    )
    token_block = lax.all_gather(attended, "sx", axis=0, tiled=True)
    weight_block = lax.all_gather(out_weight[0], "sy", axis=1, tiled=True)
    group_term = jnp.dot(token_block, weight_block, preferred_element_type=jnp.float32)
    mixed = lax.psum_scatter(
        group_term.astype(jnp.bfloat16), "head", scatter_dimension=0, tiled=True
    ).astype(jnp.float32)
    swap = linear_pairs((x_count, head_groups), lambda a, b: (b, a))
    stream_block = lax.ppermute(stream[0], ("sx", "head"), swap)
    gate_block = lax.ppermute(gate_scale[0], ("sx", "head"), swap)
    updated = (stream_block.astype(jnp.float32) + gate_block[None, :] * mixed).astype(jnp.bfloat16)
    hand = linear_pairs(
        (sections, x_count, head_groups), lambda s, a, b: ((s + 1) % sections, b, a)
    )
    handed = lax.ppermute(updated, ("section", "sx", "head"), hand)
    return handed[None]


def solution(mesh):
    sections, seq_count, head_count = mesh.devices.shape
    x_count = 4 if seq_count % 4 == 0 else 1
    split_mesh = Mesh(
        mesh.devices.reshape(sections, x_count, seq_count // x_count, head_count),
        ("section", "sx", "sy", "head"),
    )
    seq = ("sx", "sy")
    in_specs = (
        P("section", seq, "head"),
        P("section", seq, "head"),
        P("section", seq, "head"),
        P("section", seq, "head"),
        P("section", "head", seq),
        P("section", "head"),
        P(),
    )
    out_specs = P("section", seq, "head")
    return jax.shard_map(
        on_device, mesh=split_mesh, in_specs=in_specs, out_specs=out_specs, check_vma=False
    )
```

```python
from functools import partial
import math

import jax
import jax.numpy as jnp
from jax import lax
from jax.sharding import Mesh, PartitionSpec as P

HD = 128
SPATIAL = 1


def shifted(block, axis, count, distance, wanted):
    devices = range(count)
    route = [(i - distance, i) for i in devices if i - distance in devices and wanted(i)]
    return lax.ppermute(block, axis, route)


def needs(offset):
    if offset == 3:
        return lambda i: i % 2 == 1
    if offset == -3:
        return lambda i: i % 2 == 0
    return lambda i: True


def linear_pairs(sizes, mapping):
    def flat(index):
        value = 0
        for part, size in zip(index, sizes):
            value = value * size + part
        return value

    grid = [[]]
    for size in sizes:
        grid = [index + [part] for index in grid for part in range(size)]
    return [(flat(index), flat(mapping(*index))) for index in grid]


def from_behind(value, axis, steps):
    count = lax.axis_size(axis)
    pairs = [(source, (source + steps) % count) for source in range(count)]
    return lax.ppermute(value, axis, pairs)


def split_heads(slab, head_count):
    return slab.reshape(slab.shape[0], head_count, slab.shape[1] // head_count)


def tile_maxima(key_slab, head_count, spatial_count):
    parts = split_heads(key_slab, head_count).astype(jnp.float32)
    lengths = jnp.sqrt(jnp.sum(parts * parts, axis=2))
    return jnp.max(lengths.reshape(spatial_count, -1, head_count), axis=1)


def slab_keep(nearby, slab_tile, in_range, spatial_count, temporal_count):
    first = jnp.clip(slab_tile, 0, temporal_count - 1) * spatial_count
    return lax.dynamic_slice_in_dim(nearby, first, spatial_count, 1) & in_range


def attend(
    running,
    slab_entry,
    keep,
    query_parts,
    row_bound,
    head_count,
    spatial_count,
    tile_rows,
    score_scale,
):
    weighted, summed = running
    row_count = query_parts.shape[0]
    slab_keys = split_heads(slab_entry[0], head_count)
    slab_values = split_heads(slab_entry[1], head_count)
    scores = (
        jnp.einsum("qhd,khd->hqk", query_parts, slab_keys, preferred_element_type=jnp.float32)
        * score_scale
    )
    row_keep = jnp.broadcast_to(
        keep[:, None, :, None], (spatial_count, tile_rows, spatial_count, tile_rows)
    )
    row_keep = row_keep.reshape(row_count, row_count)
    weights = jnp.where(row_keep[None], jnp.exp(scores - row_bound.T[:, :, None]), 0.0)
    summed = summed + jnp.sum(weights, axis=2)
    weighted = weighted + jnp.einsum(
        "hqk,khd->qhd",
        weights.astype(jnp.bfloat16),
        slab_values,
        preferred_element_type=jnp.float32,
    )
    return (weighted, summed)


def on_device(query_heads, key_heads, value_heads, stream, out_weight, gate_scale, windows):
    queries = query_heads[0]
    own_keys = key_heads[0]
    own_values = value_heads[0]
    row_count, feature_count = queries.shape
    head_count = feature_count // HD
    spatial_count = SPATIAL
    tile_rows = row_count // spatial_count
    tile_count = windows.shape[0]
    temporal_count = tile_count // spatial_count
    score_scale = 1.0 / math.sqrt(HD)
    x_count = lax.axis_size("sx")
    y_count = lax.axis_size("sy")
    head_groups = lax.axis_size("head")
    sections = lax.axis_size("section")
    seq_count = x_count * y_count
    x_index = lax.axis_index("sx")
    y_index = lax.axis_index("sy")
    position = x_index * y_count + y_index
    temporal = position // 2
    allowed = jnp.any(
        windows[:, :, None] == jnp.arange(tile_count, dtype=jnp.int32)[None, None, :], axis=1
    )
    nearby = lax.dynamic_slice_in_dim(allowed, temporal * spatial_count, spatial_count, 0)
    always = jnp.array(True)
    slabs = [(own_keys, own_values, temporal, always)]
    reach = min(3, seq_count - 1)
    offsets = list(range(1, reach + 1)) + list(range(-reach, 0))
    for offset in offsets:
        moved_keys, moved_values = shifted(
            (own_keys, own_values), ("sx", "sy"), seq_count, offset, needs(offset)
        )
        source = position - offset
        in_range = (source >= 0) & (source < seq_count)
        slabs.append((moved_keys, moved_values, source // 2, in_range))
    keeps = [
        slab_keep(nearby, slab_entry[2], slab_entry[3], spatial_count, temporal_count)
        for slab_entry in slabs
    ]
    bound_tiles = jnp.zeros((spatial_count, head_count), jnp.float32)
    for slab_entry, keep in zip(slabs, keeps):
        maxima = tile_maxima(slab_entry[0], head_count, spatial_count)
        candidate = jnp.where(keep[:, :, None], maxima[None, :, :], 0.0)
        bound_tiles = jnp.maximum(bound_tiles, jnp.max(candidate, axis=1))
    query_parts = split_heads(queries, head_count)
    query_float = query_parts.astype(jnp.float32)
    query_lengths = jnp.sqrt(jnp.sum(query_float * query_float, axis=2))
    row_bound = query_lengths * jnp.repeat(bound_tiles, tile_rows, axis=0) * score_scale
    running = (
        jnp.zeros((row_count, head_count, HD), jnp.float32),
        jnp.zeros((head_count, row_count), jnp.float32),
    )
    for slab_entry, keep in zip(slabs, keeps):
        step_fn = partial(
            attend,
            slab_entry=slab_entry,
            keep=keep,
            query_parts=query_parts,
            row_bound=row_bound,
            head_count=head_count,
            spatial_count=spatial_count,
            tile_rows=tile_rows,
            score_scale=score_scale,
        )
        running = step_fn(running)
    weighted, summed = running
    attended = (
        (weighted / summed.T[:, :, None]).astype(jnp.bfloat16).reshape(row_count, feature_count)
    )
    weight = out_weight[0]
    forward = weight
    backward = weight
    weight_parts = {0: weight}
    for step in range(1, y_count // 2 + 1):
        forward = lax.ppermute(forward, "sy", [(i, (i + 1) % y_count) for i in range(y_count)])
        weight_parts[(-step) % y_count] = forward
        if step < y_count - step:
            backward = lax.ppermute(
                backward, "sy", [(i, (i - 1) % y_count) for i in range(y_count)]
            )
            weight_parts[step] = backward
    relative_weight = jnp.concatenate([weight_parts[r] for r in range(y_count)], axis=1)
    weight_block = jnp.roll(relative_weight, y_index * weight.shape[1], axis=1)
    token_parts = [attended] + [
        lax.ppermute(attended, "sx", [(i, (i + d) % x_count) for i in range(x_count)])
        for d in range(1, x_count)
    ]
    terms = jnp.stack(
        [
            jnp.dot(part, weight_block, preferred_element_type=jnp.float32).astype(jnp.bfloat16)
            for part in token_parts
        ]
    )
    group_index = lax.axis_index("head")
    mixed = jnp.zeros(terms.shape[1:], jnp.float32)
    for step in range(head_groups):
        pick = (x_index - group_index - step) % head_groups
        outgoing = lax.dynamic_index_in_dim(terms, pick, 0, keepdims=False)
        route = linear_pairs(
            (x_count, head_groups), lambda a, b: ((b + step) % head_groups, a)
        )
        mixed = mixed + lax.ppermute(outgoing, ("sx", "head"), route).astype(jnp.float32)
    updated = (
        stream[0].astype(jnp.float32) + gate_scale[0][None, :] * mixed
    ).astype(jnp.bfloat16)
    hand = [(s, (s + 1) % sections) for s in range(sections)]
    handed = lax.ppermute(updated, "section", hand)
    return handed[None]


def solution(mesh):
    sections, seq_count, head_count = mesh.devices.shape
    x_count = 4 if seq_count % 4 == 0 else 1
    split_mesh = Mesh(
        mesh.devices.reshape(sections, x_count, seq_count // x_count, head_count),
        ("section", "sx", "sy", "head"),
    )
    seq = ("sx", "sy")
    in_specs = (
        P("section", seq, "head"),
        P("section", seq, "head"),
        P("section", seq, "head"),
        P("section", seq, "head"),
        P("section", "head", seq),
        P("section", "head"),
        P(),
    )
    out_specs = P("section", seq, "head")
    return jax.shard_map(
        on_device, mesh=split_mesh, in_specs=in_specs, out_specs=out_specs, check_vma=False
    )
```

```python
from functools import partial
import math

import jax
import jax.numpy as jnp
from jax import lax
from jax.sharding import Mesh, PartitionSpec as P

HD = 128
SPATIAL = 1


def shifted(block, axis, count, distance, wanted):
    devices = range(count)
    route = [(i - distance, i) for i in devices if i - distance in devices and wanted(i)]
    return lax.ppermute(block, axis, route)


def needs(offset):
    if offset == 3:
        return lambda i: i % 2 == 1
    if offset == -3:
        return lambda i: i % 2 == 0
    return lambda i: True


def linear_pairs(sizes, mapping):
    def flat(index):
        value = 0
        for part, size in zip(index, sizes):
            value = value * size + part
        return value

    grid = [[]]
    for size in sizes:
        grid = [index + [part] for index in grid for part in range(size)]
    return [(flat(index), flat(mapping(*index))) for index in grid]


def from_behind(value, axis, steps):
    count = lax.axis_size(axis)
    pairs = [(source, (source + steps) % count) for source in range(count)]
    return lax.ppermute(value, axis, pairs)


def split_heads(slab, head_count):
    return slab.reshape(slab.shape[0], head_count, slab.shape[1] // head_count)


def tile_maxima(key_slab, head_count, spatial_count):
    parts = split_heads(key_slab, head_count).astype(jnp.float32)
    lengths = jnp.sqrt(jnp.sum(parts * parts, axis=2))
    return jnp.max(lengths.reshape(spatial_count, -1, head_count), axis=1)


def slab_keep(nearby, slab_tile, in_range, spatial_count, temporal_count):
    first = jnp.clip(slab_tile, 0, temporal_count - 1) * spatial_count
    return lax.dynamic_slice_in_dim(nearby, first, spatial_count, 1) & in_range


def attend(
    running,
    slab_entry,
    keep,
    query_parts,
    row_bound,
    head_count,
    spatial_count,
    tile_rows,
    score_scale,
):
    weighted, summed = running
    row_count = query_parts.shape[0]
    slab_keys = split_heads(slab_entry[0], head_count)
    slab_values = split_heads(slab_entry[1], head_count)
    scores = (
        jnp.einsum("qhd,khd->hqk", query_parts, slab_keys, preferred_element_type=jnp.float32)
        * score_scale
    )
    row_keep = jnp.broadcast_to(
        keep[:, None, :, None], (spatial_count, tile_rows, spatial_count, tile_rows)
    )
    row_keep = row_keep.reshape(row_count, row_count)
    weights = jnp.where(row_keep[None], jnp.exp(scores - row_bound.T[:, :, None]), 0.0)
    summed = summed + jnp.sum(weights, axis=2)
    weighted = weighted + jnp.einsum(
        "hqk,khd->qhd",
        weights.astype(jnp.bfloat16),
        slab_values,
        preferred_element_type=jnp.float32,
    )
    return (weighted, summed)


def on_device(query_heads, key_heads, value_heads, stream, out_weight, gate_scale, windows):
    queries = query_heads[0]
    own_keys = key_heads[0]
    own_values = value_heads[0]
    row_count, feature_count = queries.shape
    head_count = feature_count // HD
    spatial_count = SPATIAL
    tile_rows = row_count // spatial_count
    tile_count = windows.shape[0]
    temporal_count = tile_count // spatial_count
    score_scale = 1.0 / math.sqrt(HD)
    x_count = lax.axis_size("sx")
    y_count = lax.axis_size("sy")
    head_groups = lax.axis_size("head")
    sections = lax.axis_size("section")
    seq_count = x_count * y_count
    x_index = lax.axis_index("sx")
    y_index = lax.axis_index("sy")
    position = x_index * y_count + y_index
    temporal = position // 2
    allowed = jnp.any(
        windows[:, :, None] == jnp.arange(tile_count, dtype=jnp.int32)[None, None, :], axis=1
    )
    nearby = lax.dynamic_slice_in_dim(allowed, temporal * spatial_count, spatial_count, 0)
    always = jnp.array(True)
    slabs = [(own_keys, own_values, temporal, always)]
    reach = min(3, seq_count - 1)
    offsets = list(range(1, reach + 1)) + list(range(-reach, 0))
    for offset in offsets:
        moved_keys, moved_values = shifted(
            (own_keys, own_values), ("sx", "sy"), seq_count, offset, needs(offset)
        )
        source = position - offset
        in_range = (source >= 0) & (source < seq_count)
        slabs.append((moved_keys, moved_values, source // 2, in_range))
    keeps = [
        slab_keep(nearby, slab_entry[2], slab_entry[3], spatial_count, temporal_count)
        for slab_entry in slabs
    ]
    bound_tiles = jnp.zeros((spatial_count, head_count), jnp.float32)
    for slab_entry, keep in zip(slabs, keeps):
        maxima = tile_maxima(slab_entry[0], head_count, spatial_count)
        candidate = jnp.where(keep[:, :, None], maxima[None, :, :], 0.0)
        bound_tiles = jnp.maximum(bound_tiles, jnp.max(candidate, axis=1))
    query_parts = split_heads(queries, head_count)
    query_float = query_parts.astype(jnp.float32)
    query_lengths = jnp.sqrt(jnp.sum(query_float * query_float, axis=2))
    row_bound = query_lengths * jnp.repeat(bound_tiles, tile_rows, axis=0) * score_scale
    weight_block = lax.all_gather(out_weight[0], "sy", axis=1, tiled=True)
    weight_block, row_bound = lax.optimization_barrier((weight_block, row_bound))
    running = (
        jnp.zeros((row_count, head_count, HD), jnp.float32),
        jnp.zeros((head_count, row_count), jnp.float32),
    )
    for slab_entry, keep in zip(slabs, keeps):
        step_fn = partial(
            attend,
            slab_entry=slab_entry,
            keep=keep,
            query_parts=query_parts,
            row_bound=row_bound,
            head_count=head_count,
            spatial_count=spatial_count,
            tile_rows=tile_rows,
            score_scale=score_scale,
        )
        running = step_fn(running)
    weighted, summed = running
    attended = (
        (weighted / summed.T[:, :, None]).astype(jnp.bfloat16).reshape(row_count, feature_count)
    )
    token_parts = [attended] + [
        lax.ppermute(attended, "sx", [(i, (i + d) % x_count) for i in range(x_count)])
        for d in range(1, x_count)
    ]
    terms = jnp.stack(
        [
            jnp.dot(part, weight_block, preferred_element_type=jnp.float32).astype(jnp.bfloat16)
            for part in token_parts
        ]
    )
    group_index = lax.axis_index("head")

    def term_for(slab_x):
        pick = (x_index - jnp.clip(slab_x, 0, head_groups - 1)) % x_count
        return lax.dynamic_index_in_dim(terms, pick, 0, keepdims=False).astype(jnp.float32)

    last = head_groups - 1
    upward = None
    downward = None
    for step in range(1, head_groups):
        send_up = term_for(group_index + head_groups - step)
        if upward is not None:
            send_up = send_up + upward
        upward = lax.ppermute(
            send_up.astype(jnp.bfloat16), "head", [(g, g + 1) for g in range(step)]
        ).astype(jnp.float32)
        send_down = term_for(group_index - head_groups + step)
        if downward is not None:
            send_down = send_down + downward
        downward = lax.ppermute(
            send_down.astype(jnp.bfloat16),
            "head",
            [(g, g - 1) for g in range(last, last - step, -1)],
        ).astype(jnp.float32)
    mixed = term_for(group_index) + upward + downward
    swap = linear_pairs((x_count, head_groups), lambda a, b: (b, a))
    stream_block = lax.ppermute(stream[0], ("sx", "head"), swap)
    gate_block = lax.ppermute(gate_scale[0], ("sx", "head"), swap)
    updated = (stream_block.astype(jnp.float32) + gate_block[None, :] * mixed).astype(jnp.bfloat16)
    hand = linear_pairs(
        (sections, x_count, head_groups), lambda s, a, b: ((s + 1) % sections, b, a)
    )
    handed = lax.ppermute(updated, ("section", "sx", "head"), hand)
    return handed[None]


def solution(mesh):
    sections, seq_count, head_count = mesh.devices.shape
    x_count = 4 if seq_count % 4 == 0 else 1
    split_mesh = Mesh(
        mesh.devices.reshape(sections, x_count, seq_count // x_count, head_count),
        ("section", "sx", "sy", "head"),
    )
    seq = ("sx", "sy")
    in_specs = (
        P("section", seq, "head"),
        P("section", seq, "head"),
        P("section", seq, "head"),
        P("section", seq, "head"),
        P("section", "head", seq),
        P("section", "head"),
        P(),
    )
    out_specs = P("section", seq, "head")
    return jax.shard_map(
        on_device, mesh=split_mesh, in_specs=in_specs, out_specs=out_specs, check_vma=False
    )
```

```python
from functools import partial
import math

import jax
import jax.numpy as jnp
from jax import lax
from jax.sharding import Mesh, PartitionSpec as P

HD = 128
SPATIAL = 1


def shifted(block, axis, count, distance, wanted):
    devices = range(count)
    route = [(i - distance, i) for i in devices if i - distance in devices and wanted(i)]
    return lax.ppermute(block, axis, route)


def needs(offset):
    if offset == 3:
        return lambda i: i % 2 == 1
    if offset == -3:
        return lambda i: i % 2 == 0
    return lambda i: True


def linear_pairs(sizes, mapping):
    def flat(index):
        value = 0
        for part, size in zip(index, sizes):
            value = value * size + part
        return value

    grid = [[]]
    for size in sizes:
        grid = [index + [part] for index in grid for part in range(size)]
    return [(flat(index), flat(mapping(*index))) for index in grid]


def from_behind(value, axis, steps):
    count = lax.axis_size(axis)
    pairs = [(source, (source + steps) % count) for source in range(count)]
    return lax.ppermute(value, axis, pairs)


def split_heads(slab, head_count):
    return slab.reshape(slab.shape[0], head_count, slab.shape[1] // head_count)


def tile_maxima(key_slab, head_count, spatial_count):
    parts = split_heads(key_slab, head_count).astype(jnp.float32)
    lengths = jnp.sqrt(jnp.sum(parts * parts, axis=2))
    return jnp.max(lengths.reshape(spatial_count, -1, head_count), axis=1)


def slab_keep(nearby, slab_tile, in_range, spatial_count, temporal_count):
    first = jnp.clip(slab_tile, 0, temporal_count - 1) * spatial_count
    return lax.dynamic_slice_in_dim(nearby, first, spatial_count, 1) & in_range


def attend(
    running,
    slab_entry,
    keep,
    query_parts,
    row_bound,
    head_count,
    spatial_count,
    tile_rows,
    score_scale,
):
    weighted, summed = running
    row_count = query_parts.shape[0]
    slab_keys = split_heads(slab_entry[0], head_count)
    slab_values = split_heads(slab_entry[1], head_count)
    scores = (
        jnp.einsum("qhd,khd->hqk", query_parts, slab_keys, preferred_element_type=jnp.float32)
        * score_scale
    )
    row_keep = jnp.broadcast_to(
        keep[:, None, :, None], (spatial_count, tile_rows, spatial_count, tile_rows)
    )
    row_keep = row_keep.reshape(row_count, row_count)
    weights = jnp.where(row_keep[None], jnp.exp(scores - row_bound.T[:, :, None]), 0.0)
    summed = summed + jnp.sum(weights, axis=2)
    weighted = weighted + jnp.einsum(
        "hqk,khd->qhd",
        weights.astype(jnp.bfloat16),
        slab_values,
        preferred_element_type=jnp.float32,
    )
    return (weighted, summed)


def on_device(query_heads, key_heads, value_heads, stream, out_weight, gate_scale, windows):
    queries = query_heads[0]
    own_keys = key_heads[0]
    own_values = value_heads[0]
    row_count, feature_count = queries.shape
    head_count = feature_count // HD
    spatial_count = SPATIAL
    tile_rows = row_count // spatial_count
    tile_count = windows.shape[0]
    temporal_count = tile_count // spatial_count
    score_scale = 1.0 / math.sqrt(HD)
    x_count = lax.axis_size("sx")
    y_count = lax.axis_size("sy")
    head_groups = lax.axis_size("head")
    sections = lax.axis_size("section")
    seq_count = x_count * y_count
    x_index = lax.axis_index("sx")
    y_index = lax.axis_index("sy")
    position = x_index * y_count + y_index
    temporal = position // 2
    allowed = jnp.any(
        windows[:, :, None] == jnp.arange(tile_count, dtype=jnp.int32)[None, None, :], axis=1
    )
    nearby = lax.dynamic_slice_in_dim(allowed, temporal * spatial_count, spatial_count, 0)
    always = jnp.array(True)
    slabs = [(own_keys, own_values, temporal, always)]
    reach = min(3, seq_count - 1)
    offsets = list(range(1, reach + 1)) + list(range(-reach, 0))
    for offset in offsets:
        moved_keys, moved_values = shifted(
            (own_keys, own_values), ("sx", "sy"), seq_count, offset, needs(offset)
        )
        source = position - offset
        in_range = (source >= 0) & (source < seq_count)
        slabs.append((moved_keys, moved_values, source // 2, in_range))
    keeps = [
        slab_keep(nearby, slab_entry[2], slab_entry[3], spatial_count, temporal_count)
        for slab_entry in slabs
    ]
    bound_tiles = jnp.zeros((spatial_count, head_count), jnp.float32)
    for slab_entry, keep in zip(slabs, keeps):
        maxima = tile_maxima(slab_entry[0], head_count, spatial_count)
        candidate = jnp.where(keep[:, :, None], maxima[None, :, :], 0.0)
        bound_tiles = jnp.maximum(bound_tiles, jnp.max(candidate, axis=1))
    query_parts = split_heads(queries, head_count)
    query_float = query_parts.astype(jnp.float32)
    query_lengths = jnp.sqrt(jnp.sum(query_float * query_float, axis=2))
    row_bound = query_lengths * jnp.repeat(bound_tiles, tile_rows, axis=0) * score_scale
    weight_block = lax.all_gather(out_weight[0], "sy", axis=1, tiled=True)
    weight_block, row_bound = lax.optimization_barrier((weight_block, row_bound))
    running = (
        jnp.zeros((row_count, head_count, HD), jnp.float32),
        jnp.zeros((head_count, row_count), jnp.float32),
    )
    for slab_entry, keep in zip(slabs, keeps):
        step_fn = partial(
            attend,
            slab_entry=slab_entry,
            keep=keep,
            query_parts=query_parts,
            row_bound=row_bound,
            head_count=head_count,
            spatial_count=spatial_count,
            tile_rows=tile_rows,
            score_scale=score_scale,
        )
        running = step_fn(running)
    weighted, summed = running
    attended = (
        (weighted / summed.T[:, :, None]).astype(jnp.bfloat16).reshape(row_count, feature_count)
    )
    spread = jnp.broadcast_to(attended[None], (x_count,) + attended.shape)
    token_parts = lax.all_to_all(spread, "sx", 0, 0)
    terms = jnp.stack(
        [
            jnp.dot(token_parts[j], weight_block, preferred_element_type=jnp.float32).astype(
                jnp.bfloat16
            )
            for j in range(x_count)
        ]
    )
    arrived = lax.all_to_all(terms, "head", 0, 0)
    mixed = jnp.sum(arrived.astype(jnp.float32), axis=0)
    swap = linear_pairs((x_count, head_groups), lambda a, b: (b, a))
    stream_block = lax.ppermute(stream[0], ("sx", "head"), swap)
    gate_block = lax.ppermute(gate_scale[0], ("sx", "head"), swap)
    updated = (stream_block.astype(jnp.float32) + gate_block[None, :] * mixed).astype(jnp.bfloat16)
    hand = linear_pairs(
        (sections, x_count, head_groups), lambda s, a, b: ((s + 1) % sections, b, a)
    )
    handed = lax.ppermute(updated, ("section", "sx", "head"), hand)
    return handed[None]


def solution(mesh):
    sections, seq_count, head_count = mesh.devices.shape
    x_count = 4 if seq_count % 4 == 0 else 1
    split_mesh = Mesh(
        mesh.devices.reshape(sections, x_count, seq_count // x_count, head_count),
        ("section", "sx", "sy", "head"),
    )
    seq = ("sx", "sy")
    in_specs = (
        P("section", seq, "head"),
        P("section", seq, "head"),
        P("section", seq, "head"),
        P("section", seq, "head"),
        P("section", "head", seq),
        P("section", "head"),
        P(),
    )
    out_specs = P("section", seq, "head")
    return jax.shard_map(
        on_device, mesh=split_mesh, in_specs=in_specs, out_specs=out_specs, check_vma=False
    )
```

```python
from functools import partial
import math

import jax
import jax.numpy as jnp
from jax import lax
from jax.sharding import Mesh, PartitionSpec as P

HD = 128
SPATIAL = 1


def shifted(block, axis, count, distance, wanted):
    devices = range(count)
    route = [(i - distance, i) for i in devices if i - distance in devices and wanted(i)]
    return lax.ppermute(block, axis, route)


def needs(offset):
    if offset == 3:
        return lambda i: i % 2 == 1
    if offset == -3:
        return lambda i: i % 2 == 0
    return lambda i: True


def linear_pairs(sizes, mapping):
    def flat(index):
        value = 0
        for part, size in zip(index, sizes):
            value = value * size + part
        return value

    grid = [[]]
    for size in sizes:
        grid = [index + [part] for index in grid for part in range(size)]
    return [(flat(index), flat(mapping(*index))) for index in grid]


def from_behind(value, axis, steps):
    count = lax.axis_size(axis)
    pairs = [(source, (source + steps) % count) for source in range(count)]
    return lax.ppermute(value, axis, pairs)


def split_heads(slab, head_count):
    return slab.reshape(slab.shape[0], head_count, slab.shape[1] // head_count)


def tile_maxima(key_slab, head_count, spatial_count):
    parts = split_heads(key_slab, head_count).astype(jnp.float32)
    lengths = jnp.sqrt(jnp.sum(parts * parts, axis=2))
    return jnp.max(lengths.reshape(spatial_count, -1, head_count), axis=1)


def slab_keep(nearby, slab_tile, in_range, spatial_count, temporal_count):
    first = jnp.clip(slab_tile, 0, temporal_count - 1) * spatial_count
    return lax.dynamic_slice_in_dim(nearby, first, spatial_count, 1) & in_range


def attend(
    running,
    slab_entry,
    keep,
    query_parts,
    row_bound,
    head_count,
    spatial_count,
    tile_rows,
    score_scale,
):
    weighted, summed = running
    row_count = query_parts.shape[0]
    slab_keys = split_heads(slab_entry[0], head_count)
    slab_values = split_heads(slab_entry[1], head_count)
    scores = (
        jnp.einsum("qhd,khd->hqk", query_parts, slab_keys, preferred_element_type=jnp.float32)
        * score_scale
    )
    row_keep = jnp.broadcast_to(
        keep[:, None, :, None], (spatial_count, tile_rows, spatial_count, tile_rows)
    )
    row_keep = row_keep.reshape(row_count, row_count)
    weights = jnp.where(row_keep[None], jnp.exp(scores - row_bound.T[:, :, None]), 0.0)
    summed = summed + jnp.sum(weights, axis=2)
    weighted = weighted + jnp.einsum(
        "hqk,khd->qhd",
        weights.astype(jnp.bfloat16),
        slab_values,
        preferred_element_type=jnp.float32,
    )
    return (weighted, summed)


def on_device(query_heads, key_heads, value_heads, stream, out_weight, gate_scale, windows):
    queries = query_heads[0]
    own_keys = key_heads[0]
    own_values = value_heads[0]
    row_count, feature_count = queries.shape
    head_count = feature_count // HD
    spatial_count = SPATIAL
    tile_rows = row_count // spatial_count
    tile_count = windows.shape[0]
    temporal_count = tile_count // spatial_count
    score_scale = 1.0 / math.sqrt(HD)
    x_count = lax.axis_size("sx")
    y_count = lax.axis_size("sy")
    head_groups = lax.axis_size("head")
    sections = lax.axis_size("section")
    seq_count = x_count * y_count
    x_index = lax.axis_index("sx")
    y_index = lax.axis_index("sy")
    position = x_index * y_count + y_index
    parity = position % 2
    temporal = position // 2
    allowed = jnp.any(
        windows[:, :, None] == jnp.arange(tile_count, dtype=jnp.int32)[None, None, :], axis=1
    )
    row_allowed = lax.dynamic_index_in_dim(allowed, temporal, 0, keepdims=False)
    seq = ("sx", "sy")
    half = feature_count // 2
    own_heads = head_count // 2
    tile_len = 2 * row_count
    partner = [(i, i ^ 1) for i in range(seq_count)]

    def partner_half(block):
        return lax.dynamic_slice_in_dim(block, (1 - parity) * half, half, 1)

    def own_half(block):
        return lax.dynamic_slice_in_dim(block, parity * half, half, 1)

    sent = lax.ppermute(
        (partner_half(queries), partner_half(own_keys), partner_half(own_values)), seq, partner
    )

    def whole_tile(mine, theirs):
        return jnp.where(
            parity == 0,
            jnp.concatenate([mine, theirs], axis=0),
            jnp.concatenate([theirs, mine], axis=0),
        )

    tile_q = whole_tile(own_half(queries), sent[0])
    tile_k = whole_tile(own_half(own_keys), sent[1])
    tile_v = whole_tile(own_half(own_values), sent[2])
    before = lax.ppermute((tile_k, tile_v), seq, [(i, i + 2) for i in range(seq_count - 2)])
    after = lax.ppermute((tile_k, tile_v), seq, [(i, i - 2) for i in range(2, seq_count)])
    key_tiles = [before, (tile_k, tile_v), after]
    keeps = []
    for step in (-1, 0, 1):
        near = temporal + step
        in_range = (near >= 0) & (near < temporal_count)
        listed = lax.dynamic_index_in_dim(
            row_allowed, jnp.clip(near, 0, temporal_count - 1), 0, keepdims=False
        )
        keeps.append(in_range & listed)
    bound = jnp.zeros((own_heads,), jnp.float32)
    for (keys, _), keep in zip(key_tiles, keeps):
        key_float = keys.reshape(tile_len, own_heads, HD).astype(jnp.float32)
        key_lengths = jnp.sqrt(jnp.sum(key_float * key_float, axis=2))
        bound = jnp.maximum(bound, jnp.where(keep, jnp.max(key_lengths, axis=0), 0.0))
    query_parts = tile_q.reshape(tile_len, own_heads, HD)
    query_float = query_parts.astype(jnp.float32)
    query_lengths = jnp.sqrt(jnp.sum(query_float * query_float, axis=2))
    row_bound = query_lengths * bound[None, :] * score_scale
    weight_block = lax.all_gather(out_weight[0], "sy", axis=1, tiled=True)
    weight_block, row_bound = lax.optimization_barrier((weight_block, row_bound))
    weighted = jnp.zeros((tile_len, own_heads, HD), jnp.float32)
    summed = jnp.zeros((own_heads, tile_len), jnp.float32)
    for (keys, values), keep in zip(key_tiles, keeps):
        key_parts = keys.reshape(tile_len, own_heads, HD)
        value_parts = values.reshape(tile_len, own_heads, HD)
        scores = (
            jnp.einsum("qhd,khd->hqk", query_parts, key_parts, preferred_element_type=jnp.float32)
            * score_scale
        )
        weights = jnp.where(keep, jnp.exp(scores - row_bound.T[:, :, None]), 0.0)
        summed = summed + jnp.sum(weights, axis=2)
        weighted = weighted + jnp.einsum(
            "hqk,khd->qhd",
            weights.astype(jnp.bfloat16),
            value_parts,
            preferred_element_type=jnp.float32,
        )
    tile_out = (weighted / summed.T[:, :, None]).astype(jnp.bfloat16).reshape(tile_len, half)
    mine_rows = lax.dynamic_slice_in_dim(tile_out, parity * row_count, row_count, 0)
    their_rows = lax.dynamic_slice_in_dim(tile_out, (1 - parity) * row_count, row_count, 0)
    back = lax.ppermute(their_rows, seq, partner)
    attended = jnp.where(
        parity == 0,
        jnp.concatenate([mine_rows, back], axis=1),
        jnp.concatenate([back, mine_rows], axis=1),
    )
    spread = jnp.broadcast_to(attended[None], (x_count,) + attended.shape)
    token_parts = lax.all_to_all(spread, "sx", 0, 0)
    terms = jnp.stack(
        [
            jnp.dot(token_parts[j], weight_block, preferred_element_type=jnp.float32).astype(
                jnp.bfloat16
            )
            for j in range(x_count)
        ]
    )
    arrived = lax.all_to_all(terms, "head", 0, 0)
    mixed = jnp.sum(arrived.astype(jnp.float32), axis=0)
    swap = linear_pairs((x_count, head_groups), lambda a, b: (b, a))
    stream_block = lax.ppermute(stream[0], ("sx", "head"), swap)
    gate_block = lax.ppermute(gate_scale[0], ("sx", "head"), swap)
    updated = (stream_block.astype(jnp.float32) + gate_block[None, :] * mixed).astype(jnp.bfloat16)
    hand = linear_pairs(
        (sections, x_count, head_groups), lambda s, a, b: ((s + 1) % sections, b, a)
    )
    handed = lax.ppermute(updated, ("section", "sx", "head"), hand)
    return handed[None]


def solution(mesh):
    sections, seq_count, head_count = mesh.devices.shape
    x_count = 4 if seq_count % 4 == 0 else 1
    split_mesh = Mesh(
        mesh.devices.reshape(sections, x_count, seq_count // x_count, head_count),
        ("section", "sx", "sy", "head"),
    )
    seq = ("sx", "sy")
    in_specs = (
        P("section", seq, "head"),
        P("section", seq, "head"),
        P("section", seq, "head"),
        P("section", seq, "head"),
        P("section", "head", seq),
        P("section", "head"),
        P(),
    )
    out_specs = P("section", seq, "head")
    return jax.shard_map(
        on_device, mesh=split_mesh, in_specs=in_specs, out_specs=out_specs, check_vma=False
    )
```

```python
from functools import partial
import math

import jax
import jax.numpy as jnp
from jax import lax
from jax.sharding import Mesh, PartitionSpec as P

HD = 128
SPATIAL = 1


def shifted(block, axis, count, distance, wanted):
    devices = range(count)
    route = [(i - distance, i) for i in devices if i - distance in devices and wanted(i)]
    return lax.ppermute(block, axis, route)


def needs(offset):
    if offset == 3:
        return lambda i: i % 2 == 1
    if offset == -3:
        return lambda i: i % 2 == 0
    return lambda i: True


def linear_pairs(sizes, mapping):
    def flat(index):
        value = 0
        for part, size in zip(index, sizes):
            value = value * size + part
        return value

    grid = [[]]
    for size in sizes:
        grid = [index + [part] for index in grid for part in range(size)]
    return [(flat(index), flat(mapping(*index))) for index in grid]


def from_behind(value, axis, steps):
    count = lax.axis_size(axis)
    pairs = [(source, (source + steps) % count) for source in range(count)]
    return lax.ppermute(value, axis, pairs)


def split_heads(slab, head_count):
    return slab.reshape(slab.shape[0], head_count, slab.shape[1] // head_count)


def tile_maxima(key_slab, head_count, spatial_count):
    parts = split_heads(key_slab, head_count).astype(jnp.float32)
    lengths = jnp.sqrt(jnp.sum(parts * parts, axis=2))
    return jnp.max(lengths.reshape(spatial_count, -1, head_count), axis=1)


def slab_keep(nearby, slab_tile, in_range, spatial_count, temporal_count):
    first = jnp.clip(slab_tile, 0, temporal_count - 1) * spatial_count
    return lax.dynamic_slice_in_dim(nearby, first, spatial_count, 1) & in_range


def attend(
    running,
    slab_entry,
    keep,
    query_parts,
    row_bound,
    head_count,
    spatial_count,
    tile_rows,
    score_scale,
):
    weighted, summed = running
    row_count = query_parts.shape[0]
    slab_keys = split_heads(slab_entry[0], head_count)
    slab_values = split_heads(slab_entry[1], head_count)
    scores = (
        jnp.einsum("qhd,khd->hqk", query_parts, slab_keys, preferred_element_type=jnp.float32)
        * score_scale
    )
    row_keep = jnp.broadcast_to(
        keep[:, None, :, None], (spatial_count, tile_rows, spatial_count, tile_rows)
    )
    row_keep = row_keep.reshape(row_count, row_count)
    weights = jnp.where(row_keep[None], jnp.exp(scores - row_bound.T[:, :, None]), 0.0)
    summed = summed + jnp.sum(weights, axis=2)
    weighted = weighted + jnp.einsum(
        "hqk,khd->qhd",
        weights.astype(jnp.bfloat16),
        slab_values,
        preferred_element_type=jnp.float32,
    )
    return (weighted, summed)


def on_device(query_heads, key_heads, value_heads, stream, out_weight, gate_scale, windows):
    queries = query_heads[0]
    own_keys = key_heads[0]
    own_values = value_heads[0]
    row_count, feature_count = queries.shape
    head_count = feature_count // HD
    spatial_count = SPATIAL
    tile_rows = row_count // spatial_count
    tile_count = windows.shape[0]
    temporal_count = tile_count // spatial_count
    score_scale = 1.0 / math.sqrt(HD)
    x_count = lax.axis_size("sx")
    y_count = lax.axis_size("sy")
    head_groups = lax.axis_size("head")
    sections = lax.axis_size("section")
    seq_count = x_count * y_count
    x_index = lax.axis_index("sx")
    y_index = lax.axis_index("sy")
    position = x_index * y_count + y_index
    parity = position % 2
    temporal = position // 2
    allowed = jnp.any(
        windows[:, :, None] == jnp.arange(tile_count, dtype=jnp.int32)[None, None, :], axis=1
    )
    row_allowed = lax.dynamic_index_in_dim(allowed, temporal, 0, keepdims=False)
    seq = ("sx", "sy")
    half = feature_count // 2
    own_heads = head_count // 2
    tile_len = 2 * row_count
    partner = [(i, i ^ 1) for i in range(seq_count)]

    def partner_half(block):
        return lax.dynamic_slice_in_dim(block, (1 - parity) * half, half, 1)

    def own_half(block):
        return lax.dynamic_slice_in_dim(block, parity * half, half, 1)

    sent = lax.ppermute(
        (partner_half(queries), partner_half(own_keys), partner_half(own_values)), seq, partner
    )

    def whole_tile(mine, theirs):
        return jnp.where(
            parity == 0,
            jnp.concatenate([mine, theirs], axis=0),
            jnp.concatenate([theirs, mine], axis=0),
        )

    tile_q = whole_tile(own_half(queries), sent[0])
    tile_k = whole_tile(own_half(own_keys), sent[1])
    tile_v = whole_tile(own_half(own_values), sent[2])
    before = lax.ppermute((tile_k, tile_v), seq, [(i, i + 2) for i in range(seq_count - 2)])
    after = lax.ppermute((tile_k, tile_v), seq, [(i, i - 2) for i in range(2, seq_count)])
    key_tiles = [before, (tile_k, tile_v), after]
    keeps = []
    for step in (-1, 0, 1):
        near = temporal + step
        in_range = (near >= 0) & (near < temporal_count)
        listed = lax.dynamic_index_in_dim(
            row_allowed, jnp.clip(near, 0, temporal_count - 1), 0, keepdims=False
        )
        keeps.append(in_range & listed)
    bound = jnp.zeros((own_heads,), jnp.float32)
    for (keys, _), keep in zip(key_tiles, keeps):
        key_float = keys.reshape(tile_len, own_heads, HD).astype(jnp.float32)
        key_lengths = jnp.sqrt(jnp.sum(key_float * key_float, axis=2))
        bound = jnp.maximum(bound, jnp.where(keep, jnp.max(key_lengths, axis=0), 0.0))
    query_parts = tile_q.reshape(tile_len, own_heads, HD)
    query_float = query_parts.astype(jnp.float32)
    query_lengths = jnp.sqrt(jnp.sum(query_float * query_float, axis=2))
    row_bound = query_lengths * bound[None, :] * score_scale
    weight_block = lax.all_gather(out_weight[0], "sy", axis=1, tiled=True)
    weight_block, row_bound = lax.optimization_barrier((weight_block, row_bound))
    weighted = jnp.zeros((tile_len, own_heads, HD), jnp.float32)
    summed = jnp.zeros((own_heads, tile_len), jnp.float32)
    for (keys, values), keep in zip(key_tiles, keeps):
        key_parts = keys.reshape(tile_len, own_heads, HD)
        value_parts = values.reshape(tile_len, own_heads, HD)
        scores = (
            jnp.einsum("qhd,khd->hqk", query_parts, key_parts, preferred_element_type=jnp.float32)
            * score_scale
        )
        weights = jnp.where(keep, jnp.exp(scores - row_bound.T[:, :, None]), 0.0)
        summed = summed + jnp.sum(weights, axis=2)
        weighted = weighted + jnp.einsum(
            "hqk,khd->qhd",
            weights.astype(jnp.bfloat16),
            value_parts,
            preferred_element_type=jnp.float32,
        )
    tile_out = (weighted / summed.T[:, :, None]).astype(jnp.bfloat16).reshape(tile_len, half)
    mine_rows = lax.dynamic_slice_in_dim(tile_out, parity * row_count, row_count, 0)
    their_rows = lax.dynamic_slice_in_dim(tile_out, (1 - parity) * row_count, row_count, 0)
    back = lax.ppermute(their_rows, seq, partner)
    attended = jnp.where(
        parity == 0,
        jnp.concatenate([mine_rows, back], axis=1),
        jnp.concatenate([back, mine_rows], axis=1),
    )
    up_ring = [(i, (i + 1) % x_count) for i in range(x_count)]
    down_ring = [(i, (i - 1) % x_count) for i in range(x_count)]
    from_below = lax.ppermute(attended, "sx", up_ring)
    from_above = lax.ppermute(attended, "sx", down_ring)
    middle = row_count // 2
    far = jnp.concatenate(
        [
            lax.ppermute(from_below[:middle], "sx", up_ring),
            lax.ppermute(from_above[middle:], "sx", down_ring),
        ],
        axis=0,
    )
    relative = [attended, from_below, far, from_above]
    relative_terms = jnp.stack(
        [
            jnp.dot(part, weight_block, preferred_element_type=jnp.float32).astype(jnp.bfloat16)
            for part in relative
        ]
    )
    terms = jnp.take(relative_terms, (x_index - jnp.arange(x_count)) % x_count, axis=0)
    arrived = lax.all_to_all(terms, "head", 0, 0)
    mixed = jnp.sum(arrived.astype(jnp.float32), axis=0)
    swap = linear_pairs((x_count, head_groups), lambda a, b: (b, a))
    stream_block = lax.ppermute(stream[0], ("sx", "head"), swap)
    gate_block = lax.ppermute(gate_scale[0], ("sx", "head"), swap)
    updated = (stream_block.astype(jnp.float32) + gate_block[None, :] * mixed).astype(jnp.bfloat16)
    hand = linear_pairs(
        (sections, x_count, head_groups), lambda s, a, b: ((s + 1) % sections, b, a)
    )
    handed = lax.ppermute(updated, ("section", "sx", "head"), hand)
    return handed[None]


def solution(mesh):
    sections, seq_count, head_count = mesh.devices.shape
    x_count = 4 if seq_count % 4 == 0 else 1
    split_mesh = Mesh(
        mesh.devices.reshape(sections, x_count, seq_count // x_count, head_count),
        ("section", "sx", "sy", "head"),
    )
    seq = ("sx", "sy")
    in_specs = (
        P("section", seq, "head"),
        P("section", seq, "head"),
        P("section", seq, "head"),
        P("section", seq, "head"),
        P("section", "head", seq),
        P("section", "head"),
        P(),
    )
    out_specs = P("section", seq, "head")
    return jax.shard_map(
        on_device, mesh=split_mesh, in_specs=in_specs, out_specs=out_specs, check_vma=False
    )
```

```python
from functools import partial
import math

import jax
import jax.numpy as jnp
from jax import lax
from jax.sharding import Mesh, PartitionSpec as P

HD = 128
SPATIAL = 1


def shifted(block, axis, count, distance, wanted):
    devices = range(count)
    route = [(i - distance, i) for i in devices if i - distance in devices and wanted(i)]
    return lax.ppermute(block, axis, route)


def needs(offset):
    if offset == 3:
        return lambda i: i % 2 == 1
    if offset == -3:
        return lambda i: i % 2 == 0
    return lambda i: True


def linear_pairs(sizes, mapping):
    def flat(index):
        value = 0
        for part, size in zip(index, sizes):
            value = value * size + part
        return value

    grid = [[]]
    for size in sizes:
        grid = [index + [part] for index in grid for part in range(size)]
    return [(flat(index), flat(mapping(*index))) for index in grid]


def from_behind(value, axis, steps):
    count = lax.axis_size(axis)
    pairs = [(source, (source + steps) % count) for source in range(count)]
    return lax.ppermute(value, axis, pairs)


def split_heads(slab, head_count):
    return slab.reshape(slab.shape[0], head_count, slab.shape[1] // head_count)


def tile_maxima(key_slab, head_count, spatial_count):
    parts = split_heads(key_slab, head_count).astype(jnp.float32)
    lengths = jnp.sqrt(jnp.sum(parts * parts, axis=2))
    return jnp.max(lengths.reshape(spatial_count, -1, head_count), axis=1)


def slab_keep(nearby, slab_tile, in_range, spatial_count, temporal_count):
    first = jnp.clip(slab_tile, 0, temporal_count - 1) * spatial_count
    return lax.dynamic_slice_in_dim(nearby, first, spatial_count, 1) & in_range


def attend(
    running,
    slab_entry,
    keep,
    query_parts,
    row_bound,
    head_count,
    spatial_count,
    tile_rows,
    score_scale,
):
    weighted, summed = running
    row_count = query_parts.shape[0]
    slab_keys = split_heads(slab_entry[0], head_count)
    slab_values = split_heads(slab_entry[1], head_count)
    scores = (
        jnp.einsum("qhd,khd->hqk", query_parts, slab_keys, preferred_element_type=jnp.float32)
        * score_scale
    )
    row_keep = jnp.broadcast_to(
        keep[:, None, :, None], (spatial_count, tile_rows, spatial_count, tile_rows)
    )
    row_keep = row_keep.reshape(row_count, row_count)
    weights = jnp.where(row_keep[None], jnp.exp(scores - row_bound.T[:, :, None]), 0.0)
    summed = summed + jnp.sum(weights, axis=2)
    weighted = weighted + jnp.einsum(
        "hqk,khd->qhd",
        weights.astype(jnp.bfloat16),
        slab_values,
        preferred_element_type=jnp.float32,
    )
    return (weighted, summed)


def on_device(query_heads, key_heads, value_heads, stream, out_weight, gate_scale, windows):
    queries = query_heads[0]
    own_keys = key_heads[0]
    own_values = value_heads[0]
    row_count, feature_count = queries.shape
    head_count = feature_count // HD
    spatial_count = SPATIAL
    tile_rows = row_count // spatial_count
    tile_count = windows.shape[0]
    temporal_count = tile_count // spatial_count
    score_scale = 1.0 / math.sqrt(HD)
    x_count = lax.axis_size("sx")
    y_count = lax.axis_size("sy")
    head_groups = lax.axis_size("head")
    sections = lax.axis_size("section")
    seq_count = x_count * y_count
    x_index = lax.axis_index("sx")
    y_index = lax.axis_index("sy")
    position = x_index * y_count + y_index
    parity = position % 2
    temporal = position // 2
    allowed = jnp.any(
        windows[:, :, None] == jnp.arange(tile_count, dtype=jnp.int32)[None, None, :], axis=1
    )
    row_allowed = lax.dynamic_index_in_dim(allowed, temporal, 0, keepdims=False)
    seq = ("sx", "sy")
    half = feature_count // 2
    own_heads = head_count // 2
    tile_len = 2 * row_count
    partner = [(i, i ^ 1) for i in range(seq_count)]

    def partner_half(block):
        return lax.dynamic_slice_in_dim(block, (1 - parity) * half, half, 1)

    def own_half(block):
        return lax.dynamic_slice_in_dim(block, parity * half, half, 1)

    swapped = lax.ppermute(
        jnp.concatenate(
            [partner_half(queries), partner_half(own_keys), partner_half(own_values)], axis=1
        ),
        seq,
        partner,
    )
    sent = [swapped[:, part * half:(part + 1) * half] for part in range(3)]

    def whole_tile(mine, theirs):
        return jnp.where(
            parity == 0,
            jnp.concatenate([mine, theirs], axis=0),
            jnp.concatenate([theirs, mine], axis=0),
        )

    tile_q = whole_tile(own_half(queries), sent[0])
    tile_k = whole_tile(own_half(own_keys), sent[1])
    tile_v = whole_tile(own_half(own_values), sent[2])
    halves = [
        jnp.concatenate(
            [own_keys[:, r * half:(r + 1) * half], own_values[:, r * half:(r + 1) * half]],
            axis=1,
        )
        for r in range(2)
    ]
    near_slabs = {}
    for offset in (-2, -1, 2, 3):
        arrived = []
        for r in range(2):
            route = [
                (2 * t + offset, 2 * t + r)
                for t in range(seq_count // 2)
                if 0 <= 2 * t + offset < seq_count
            ]
            arrived.append(lax.ppermute(halves[r], seq, route))
        near_slabs[offset] = jnp.where(parity == 0, arrived[0], arrived[1])

    def near_tile(first, second):
        keys = jnp.concatenate([near_slabs[first][:, :half], near_slabs[second][:, :half]], 0)
        values = jnp.concatenate(
            [near_slabs[first][:, half:], near_slabs[second][:, half:]], 0
        )
        return keys, values

    before = near_tile(-2, -1)
    after = near_tile(2, 3)
    key_tiles = [before, (tile_k, tile_v), after]
    keeps = []
    for step in (-1, 0, 1):
        near = temporal + step
        in_range = (near >= 0) & (near < temporal_count)
        listed = lax.dynamic_index_in_dim(
            row_allowed, jnp.clip(near, 0, temporal_count - 1), 0, keepdims=False
        )
        keeps.append(in_range & listed)
    bound = jnp.zeros((own_heads,), jnp.float32)
    for (keys, _), keep in zip(key_tiles, keeps):
        key_float = keys.reshape(tile_len, own_heads, HD).astype(jnp.float32)
        key_lengths = jnp.sqrt(jnp.sum(key_float * key_float, axis=2))
        bound = jnp.maximum(bound, jnp.where(keep, jnp.max(key_lengths, axis=0), 0.0))
    query_parts = tile_q.reshape(tile_len, own_heads, HD)
    query_float = query_parts.astype(jnp.float32)
    query_lengths = jnp.sqrt(jnp.sum(query_float * query_float, axis=2))
    row_bound = query_lengths * bound[None, :] * score_scale
    weight_block = lax.all_gather(out_weight[0], "sy", axis=1, tiled=True)
    weight_block, row_bound = lax.optimization_barrier((weight_block, row_bound))
    weighted = jnp.zeros((tile_len, own_heads, HD), jnp.float32)
    summed = jnp.zeros((own_heads, tile_len), jnp.float32)
    for (keys, values), keep in zip(key_tiles, keeps):
        key_parts = keys.reshape(tile_len, own_heads, HD)
        value_parts = values.reshape(tile_len, own_heads, HD)
        scores = (
            jnp.einsum("qhd,khd->hqk", query_parts, key_parts, preferred_element_type=jnp.float32)
            * score_scale
        )
        weights = jnp.where(keep, jnp.exp(scores - row_bound.T[:, :, None]), 0.0)
        summed = summed + jnp.sum(weights, axis=2)
        weighted = weighted + jnp.einsum(
            "hqk,khd->qhd",
            weights.astype(jnp.bfloat16),
            value_parts,
            preferred_element_type=jnp.float32,
        )
    tile_out = (weighted / summed.T[:, :, None]).astype(jnp.bfloat16).reshape(tile_len, half)
    mine_rows = lax.dynamic_slice_in_dim(tile_out, parity * row_count, row_count, 0)
    their_rows = lax.dynamic_slice_in_dim(tile_out, (1 - parity) * row_count, row_count, 0)
    back = lax.ppermute(their_rows, seq, partner)
    attended = jnp.where(
        parity == 0,
        jnp.concatenate([mine_rows, back], axis=1),
        jnp.concatenate([back, mine_rows], axis=1),
    )
    spread = jnp.broadcast_to(attended[None], (x_count,) + attended.shape)
    token_parts = lax.all_to_all(spread, "sx", 0, 0)
    terms = jnp.stack(
        [
            jnp.dot(token_parts[j], weight_block, preferred_element_type=jnp.float32).astype(
                jnp.bfloat16
            )
            for j in range(x_count)
        ]
    )
    arrived = lax.all_to_all(terms, "head", 0, 0)
    mixed = jnp.sum(arrived.astype(jnp.float32), axis=0)
    swap = linear_pairs((x_count, head_groups), lambda a, b: (b, a))
    stream_block = lax.ppermute(stream[0], ("sx", "head"), swap)
    gate_block = lax.ppermute(gate_scale[0], ("sx", "head"), swap)
    updated = (stream_block.astype(jnp.float32) + gate_block[None, :] * mixed).astype(jnp.bfloat16)
    hand = linear_pairs(
        (sections, x_count, head_groups), lambda s, a, b: ((s + 1) % sections, b, a)
    )
    handed = lax.ppermute(updated, ("section", "sx", "head"), hand)
    return handed[None]


def solution(mesh):
    sections, seq_count, head_count = mesh.devices.shape
    x_count = 4 if seq_count % 4 == 0 else 1
    split_mesh = Mesh(
        mesh.devices.reshape(sections, x_count, seq_count // x_count, head_count),
        ("section", "sx", "sy", "head"),
    )
    seq = ("sx", "sy")
    in_specs = (
        P("section", seq, "head"),
        P("section", seq, "head"),
        P("section", seq, "head"),
        P("section", seq, "head"),
        P("section", "head", seq),
        P("section", "head"),
        P(),
    )
    out_specs = P("section", seq, "head")
    return jax.shard_map(
        on_device, mesh=split_mesh, in_specs=in_specs, out_specs=out_specs, check_vma=False
    )
```

```python
from functools import partial
import math

import jax
import jax.numpy as jnp
from jax import lax
from jax.sharding import Mesh, PartitionSpec as P

HD = 128
SPATIAL = 1


def shifted(block, axis, count, distance, wanted):
    devices = range(count)
    route = [(i - distance, i) for i in devices if i - distance in devices and wanted(i)]
    return lax.ppermute(block, axis, route)


def needs(offset):
    if offset == 3:
        return lambda i: i % 2 == 1
    if offset == -3:
        return lambda i: i % 2 == 0
    return lambda i: True


def linear_pairs(sizes, mapping):
    def flat(index):
        value = 0
        for part, size in zip(index, sizes):
            value = value * size + part
        return value

    grid = [[]]
    for size in sizes:
        grid = [index + [part] for index in grid for part in range(size)]
    return [(flat(index), flat(mapping(*index))) for index in grid]


def from_behind(value, axis, steps):
    count = lax.axis_size(axis)
    pairs = [(source, (source + steps) % count) for source in range(count)]
    return lax.ppermute(value, axis, pairs)


def split_heads(slab, head_count):
    return slab.reshape(slab.shape[0], head_count, slab.shape[1] // head_count)


def tile_maxima(key_slab, head_count, spatial_count):
    parts = split_heads(key_slab, head_count).astype(jnp.float32)
    lengths = jnp.sqrt(jnp.sum(parts * parts, axis=2))
    return jnp.max(lengths.reshape(spatial_count, -1, head_count), axis=1)


def slab_keep(nearby, slab_tile, in_range, spatial_count, temporal_count):
    first = jnp.clip(slab_tile, 0, temporal_count - 1) * spatial_count
    return lax.dynamic_slice_in_dim(nearby, first, spatial_count, 1) & in_range


def attend(
    running,
    slab_entry,
    keep,
    query_parts,
    row_bound,
    head_count,
    spatial_count,
    tile_rows,
    score_scale,
):
    weighted, summed = running
    row_count = query_parts.shape[0]
    slab_keys = split_heads(slab_entry[0], head_count)
    slab_values = split_heads(slab_entry[1], head_count)
    scores = (
        jnp.einsum("qhd,khd->hqk", query_parts, slab_keys, preferred_element_type=jnp.float32)
        * score_scale
    )
    row_keep = jnp.broadcast_to(
        keep[:, None, :, None], (spatial_count, tile_rows, spatial_count, tile_rows)
    )
    row_keep = row_keep.reshape(row_count, row_count)
    weights = jnp.where(row_keep[None], jnp.exp(scores - row_bound.T[:, :, None]), 0.0)
    summed = summed + jnp.sum(weights, axis=2)
    weighted = weighted + jnp.einsum(
        "hqk,khd->qhd",
        weights.astype(jnp.bfloat16),
        slab_values,
        preferred_element_type=jnp.float32,
    )
    return (weighted, summed)


def on_device(query_heads, key_heads, value_heads, stream, out_weight, gate_scale, windows):
    queries = query_heads[0]
    own_keys = key_heads[0]
    own_values = value_heads[0]
    row_count, feature_count = queries.shape
    head_count = feature_count // HD
    spatial_count = SPATIAL
    tile_rows = row_count // spatial_count
    tile_count = windows.shape[0]
    temporal_count = tile_count // spatial_count
    score_scale = 1.0 / math.sqrt(HD)
    x_count = lax.axis_size("sxhi") * lax.axis_size("sxlo")
    y_count = lax.axis_size("sy")
    head_groups = lax.axis_size("head")
    sections = lax.axis_size("section")
    seq_count = x_count * y_count
    pair_index = lax.axis_index("sxlo")
    x_index = lax.axis_index("sxhi") * lax.axis_size("sxlo") + pair_index
    y_index = lax.axis_index("sy")
    position = x_index * y_count + y_index
    parity = position % 2
    temporal = position // 2
    allowed = jnp.any(
        windows[:, :, None] == jnp.arange(tile_count, dtype=jnp.int32)[None, None, :], axis=1
    )
    row_allowed = lax.dynamic_index_in_dim(allowed, temporal, 0, keepdims=False)
    seq = ("sxhi", "sxlo", "sy")
    half = feature_count // 2
    own_heads = head_count // 2
    tile_len = 2 * row_count
    partner = [(i, i ^ 1) for i in range(seq_count)]

    def partner_half(block):
        return lax.dynamic_slice_in_dim(block, (1 - parity) * half, half, 1)

    def own_half(block):
        return lax.dynamic_slice_in_dim(block, parity * half, half, 1)

    sent = lax.ppermute(
        (partner_half(queries), partner_half(own_keys), partner_half(own_values)), seq, partner
    )

    def whole_tile(mine, theirs):
        return jnp.where(
            parity == 0,
            jnp.concatenate([mine, theirs], axis=0),
            jnp.concatenate([theirs, mine], axis=0),
        )

    tile_q = whole_tile(own_half(queries), sent[0])
    tile_k = whole_tile(own_half(own_keys), sent[1])
    tile_v = whole_tile(own_half(own_values), sent[2])
    before = lax.ppermute((tile_k, tile_v), seq, [(i, i + 2) for i in range(seq_count - 2)])
    after = lax.ppermute((tile_k, tile_v), seq, [(i, i - 2) for i in range(2, seq_count)])
    key_tiles = [before, (tile_k, tile_v), after]
    keeps = []
    for step in (-1, 0, 1):
        near = temporal + step
        in_range = (near >= 0) & (near < temporal_count)
        listed = lax.dynamic_index_in_dim(
            row_allowed, jnp.clip(near, 0, temporal_count - 1), 0, keepdims=False
        )
        keeps.append(in_range & listed)
    bound = jnp.zeros((own_heads,), jnp.float32)
    for (keys, _), keep in zip(key_tiles, keeps):
        key_float = keys.reshape(tile_len, own_heads, HD).astype(jnp.float32)
        key_lengths = jnp.sqrt(jnp.sum(key_float * key_float, axis=2))
        bound = jnp.maximum(bound, jnp.where(keep, jnp.max(key_lengths, axis=0), 0.0))
    query_parts = tile_q.reshape(tile_len, own_heads, HD)
    query_float = query_parts.astype(jnp.float32)
    query_lengths = jnp.sqrt(jnp.sum(query_float * query_float, axis=2))
    row_bound = query_lengths * bound[None, :] * score_scale
    weight_block = lax.all_gather(out_weight[0], ("sxhi", "sy"), axis=1, tiled=True)
    weight_block, row_bound = lax.optimization_barrier((weight_block, row_bound))
    weighted = jnp.zeros((tile_len, own_heads, HD), jnp.float32)
    summed = jnp.zeros((own_heads, tile_len), jnp.float32)
    for (keys, values), keep in zip(key_tiles, keeps):
        key_parts = keys.reshape(tile_len, own_heads, HD)
        value_parts = values.reshape(tile_len, own_heads, HD)
        scores = (
            jnp.einsum("qhd,khd->hqk", query_parts, key_parts, preferred_element_type=jnp.float32)
            * score_scale
        )
        weights = jnp.where(keep, jnp.exp(scores - row_bound.T[:, :, None]), 0.0)
        summed = summed + jnp.sum(weights, axis=2)
        weighted = weighted + jnp.einsum(
            "hqk,khd->qhd",
            weights.astype(jnp.bfloat16),
            value_parts,
            preferred_element_type=jnp.float32,
        )
    tile_out = (weighted / summed.T[:, :, None]).astype(jnp.bfloat16).reshape(tile_len, half)
    mine_rows = lax.dynamic_slice_in_dim(tile_out, parity * row_count, row_count, 0)
    their_rows = lax.dynamic_slice_in_dim(tile_out, (1 - parity) * row_count, row_count, 0)
    back = lax.ppermute(their_rows, seq, partner)
    attended = jnp.where(
        parity == 0,
        jnp.concatenate([mine_rows, back], axis=1),
        jnp.concatenate([back, mine_rows], axis=1),
    )
    other = lax.ppermute(attended, "sxlo", [(0, 1), (1, 0)])
    slab_of = [jnp.where(pair_index == a, attended, other) for a in range(2)]
    columns = weight_block.shape[1] // 2
    terms = jnp.stack(
        [
            jnp.dot(
                slab_of[a],
                weight_block[:, b * columns:(b + 1) * columns],
                preferred_element_type=jnp.float32,
            ).astype(jnp.bfloat16)
            for a in range(2)
            for b in range(2)
        ]
    )
    arrived = lax.all_to_all(terms, "head", 0, 0)
    mixed = jnp.sum(arrived.astype(jnp.float32), axis=0)
    fetch = linear_pairs((2, head_groups), lambda a, c: (c % 2, 2 * a + c // 2))
    stream_block = lax.ppermute(stream[0], ("sxlo", "head"), fetch)
    gate_block = lax.ppermute(gate_scale[0], ("sxlo", "head"), fetch)
    updated = (stream_block.astype(jnp.float32) + gate_block[None, :] * mixed).astype(jnp.bfloat16)
    hand = linear_pairs(
        (sections, 2, head_groups),
        lambda s, l, g: ((s + 1) % sections, g // 2, l + 2 * (g % 2)),
    )
    handed = lax.ppermute(updated, ("section", "sxlo", "head"), hand)
    return handed[None]


def solution(mesh):
    sections, seq_count, head_count = mesh.devices.shape
    x_count = 4 if seq_count % 4 == 0 else 1
    split_mesh = Mesh(
        mesh.devices.reshape(sections, x_count // 2, 2, seq_count // x_count, head_count),
        ("section", "sxhi", "sxlo", "sy", "head"),
    )
    seq = ("sxhi", "sxlo", "sy")
    in_specs = (
        P("section", seq, "head"),
        P("section", seq, "head"),
        P("section", seq, "head"),
        P("section", seq, "head"),
        P("section", "head", seq),
        P("section", "head"),
        P(),
    )
    out_specs = P("section", seq, "head")
    return jax.shard_map(
        on_device, mesh=split_mesh, in_specs=in_specs, out_specs=out_specs, check_vma=False
    )
```

```python
from functools import partial
import math

import jax
import jax.numpy as jnp
from jax import lax
from jax.sharding import Mesh, PartitionSpec as P

HD = 128
SPATIAL = 1


def shifted(block, axis, count, distance, wanted):
    devices = range(count)
    route = [(i - distance, i) for i in devices if i - distance in devices and wanted(i)]
    return lax.ppermute(block, axis, route)


def needs(offset):
    if offset == 3:
        return lambda i: i % 2 == 1
    if offset == -3:
        return lambda i: i % 2 == 0
    return lambda i: True


def linear_pairs(sizes, mapping):
    def flat(index):
        value = 0
        for part, size in zip(index, sizes):
            value = value * size + part
        return value

    grid = [[]]
    for size in sizes:
        grid = [index + [part] for index in grid for part in range(size)]
    return [(flat(index), flat(mapping(*index))) for index in grid]


def from_behind(value, axis, steps):
    count = lax.axis_size(axis)
    pairs = [(source, (source + steps) % count) for source in range(count)]
    return lax.ppermute(value, axis, pairs)


def split_heads(slab, head_count):
    return slab.reshape(slab.shape[0], head_count, slab.shape[1] // head_count)


def tile_maxima(key_slab, head_count, spatial_count):
    parts = split_heads(key_slab, head_count).astype(jnp.float32)
    lengths = jnp.sqrt(jnp.sum(parts * parts, axis=2))
    return jnp.max(lengths.reshape(spatial_count, -1, head_count), axis=1)


def slab_keep(nearby, slab_tile, in_range, spatial_count, temporal_count):
    first = jnp.clip(slab_tile, 0, temporal_count - 1) * spatial_count
    return lax.dynamic_slice_in_dim(nearby, first, spatial_count, 1) & in_range


def attend(
    running,
    slab_entry,
    keep,
    query_parts,
    row_bound,
    head_count,
    spatial_count,
    tile_rows,
    score_scale,
):
    weighted, summed = running
    row_count = query_parts.shape[0]
    slab_keys = split_heads(slab_entry[0], head_count)
    slab_values = split_heads(slab_entry[1], head_count)
    scores = (
        jnp.einsum("qhd,khd->hqk", query_parts, slab_keys, preferred_element_type=jnp.float32)
        * score_scale
    )
    row_keep = jnp.broadcast_to(
        keep[:, None, :, None], (spatial_count, tile_rows, spatial_count, tile_rows)
    )
    row_keep = row_keep.reshape(row_count, row_count)
    weights = jnp.where(row_keep[None], jnp.exp(scores - row_bound.T[:, :, None]), 0.0)
    summed = summed + jnp.sum(weights, axis=2)
    weighted = weighted + jnp.einsum(
        "hqk,khd->qhd",
        weights.astype(jnp.bfloat16),
        slab_values,
        preferred_element_type=jnp.float32,
    )
    return (weighted, summed)


def on_device(query_heads, key_heads, value_heads, stream, out_weight, gate_scale, windows):
    queries = query_heads[0]
    own_keys = key_heads[0]
    own_values = value_heads[0]
    row_count, feature_count = queries.shape
    head_count = feature_count // HD
    spatial_count = SPATIAL
    tile_rows = row_count // spatial_count
    tile_count = windows.shape[0]
    temporal_count = tile_count // spatial_count
    score_scale = 1.0 / math.sqrt(HD)
    x_count = lax.axis_size("sx")
    y_count = lax.axis_size("sy")
    head_groups = lax.axis_size("head")
    sections = lax.axis_size("section")
    seq_count = x_count * y_count
    x_index = lax.axis_index("sx")
    y_index = lax.axis_index("sy")
    position = x_index * y_count + y_index
    parity = position % 2
    temporal = position // 2
    allowed = jnp.any(
        windows[:, :, None] == jnp.arange(tile_count, dtype=jnp.int32)[None, None, :], axis=1
    )
    row_allowed = lax.dynamic_index_in_dim(allowed, temporal, 0, keepdims=False)
    seq = ("sx", "sy")
    half = feature_count // 2
    own_heads = head_count // 2
    tile_len = 2 * row_count
    partner = [(i, i ^ 1) for i in range(seq_count)]

    def partner_half(block):
        return lax.dynamic_slice_in_dim(block, (1 - parity) * half, half, 1)

    def own_half(block):
        return lax.dynamic_slice_in_dim(block, parity * half, half, 1)

    sent = lax.ppermute(
        (partner_half(queries), partner_half(own_keys), partner_half(own_values)), seq, partner
    )

    def whole_tile(mine, theirs):
        return jnp.where(
            parity == 0,
            jnp.concatenate([mine, theirs], axis=0),
            jnp.concatenate([theirs, mine], axis=0),
        )

    tile_q = whole_tile(own_half(queries), sent[0])
    tile_k = whole_tile(own_half(own_keys), sent[1])
    tile_v = whole_tile(own_half(own_values), sent[2])
    before = lax.ppermute((tile_k, tile_v), seq, [(i, i + 2) for i in range(seq_count - 2)])
    after = lax.ppermute((tile_k, tile_v), seq, [(i, i - 2) for i in range(2, seq_count)])
    key_tiles = [before, (tile_k, tile_v), after]
    keeps = []
    for step in (-1, 0, 1):
        near = temporal + step
        in_range = (near >= 0) & (near < temporal_count)
        listed = lax.dynamic_index_in_dim(
            row_allowed, jnp.clip(near, 0, temporal_count - 1), 0, keepdims=False
        )
        keeps.append(in_range & listed)
    bound = jnp.zeros((own_heads,), jnp.float32)
    for (keys, _), keep in zip(key_tiles, keeps):
        key_float = keys.reshape(tile_len, own_heads, HD).astype(jnp.float32)
        key_lengths = jnp.sqrt(jnp.sum(key_float * key_float, axis=2))
        bound = jnp.maximum(bound, jnp.where(keep, jnp.max(key_lengths, axis=0), 0.0))
    query_parts = tile_q.reshape(tile_len, own_heads, HD)
    query_float = query_parts.astype(jnp.float32)
    query_lengths = jnp.sqrt(jnp.sum(query_float * query_float, axis=2))
    row_bound = query_lengths * bound[None, :] * score_scale
    weight_block = lax.all_gather(out_weight[0], "sy", axis=1, tiled=True)
    weight_block, row_bound = lax.optimization_barrier((weight_block, row_bound))
    weighted = jnp.zeros((tile_len, own_heads, HD), jnp.float32)
    summed = jnp.zeros((own_heads, tile_len), jnp.float32)
    for (keys, values), keep in zip(key_tiles, keeps):
        key_parts = keys.reshape(tile_len, own_heads, HD)
        value_parts = values.reshape(tile_len, own_heads, HD)
        scores = (
            jnp.einsum("qhd,khd->hqk", query_parts, key_parts, preferred_element_type=jnp.float32)
            * score_scale
        )
        weights = jnp.where(keep, jnp.exp(scores - row_bound.T[:, :, None]), 0.0)
        summed = summed + jnp.sum(weights, axis=2)
        weighted = weighted + jnp.einsum(
            "hqk,khd->qhd",
            weights.astype(jnp.bfloat16),
            value_parts,
            preferred_element_type=jnp.float32,
        )
    tile_out = (weighted / summed.T[:, :, None]).astype(jnp.bfloat16).reshape(tile_len, half)
    mine_rows = lax.dynamic_slice_in_dim(tile_out, parity * row_count, row_count, 0)
    their_rows = lax.dynamic_slice_in_dim(tile_out, (1 - parity) * row_count, row_count, 0)
    back = lax.ppermute(their_rows, seq, partner)
    attended = jnp.where(
        parity == 0,
        jnp.concatenate([mine_rows, back], axis=1),
        jnp.concatenate([back, mine_rows], axis=1),
    )
    swap = linear_pairs((x_count, head_groups), lambda a, b: (b, a))
    stream_block = lax.ppermute(stream[0], ("sx", "head"), swap)
    gate_block = lax.ppermute(gate_scale[0], ("sx", "head"), swap)
    hand = linear_pairs(
        (sections, x_count, head_groups), lambda s, a, b: ((s + 1) % sections, b, a)
    )
    chunk_rows = row_count // 2
    handed_chunks = []
    for chunk in range(2):
        rows = slice(chunk * chunk_rows, (chunk + 1) * chunk_rows)
        piece = attended[rows]
        spread = jnp.broadcast_to(piece[None], (x_count,) + piece.shape)
        token_parts = lax.all_to_all(spread, "sx", 0, 0)
        terms = jnp.stack(
            [
                jnp.dot(
                    token_parts[j], weight_block, preferred_element_type=jnp.float32
                ).astype(jnp.bfloat16)
                for j in range(x_count)
            ]
        )
        arrived = lax.all_to_all(terms, "head", 0, 0)
        mixed = jnp.sum(arrived.astype(jnp.float32), axis=0)
        updated = (
            stream_block[rows].astype(jnp.float32) + gate_block[None, :] * mixed
        ).astype(jnp.bfloat16)
        handed_chunks.append(lax.ppermute(updated, ("section", "sx", "head"), hand))
    handed = jnp.concatenate(handed_chunks, axis=0)
    return handed[None]


def solution(mesh):
    sections, seq_count, head_count = mesh.devices.shape
    x_count = 4 if seq_count % 4 == 0 else 1
    split_mesh = Mesh(
        mesh.devices.reshape(sections, x_count, seq_count // x_count, head_count),
        ("section", "sx", "sy", "head"),
    )
    seq = ("sx", "sy")
    in_specs = (
        P("section", seq, "head"),
        P("section", seq, "head"),
        P("section", seq, "head"),
        P("section", seq, "head"),
        P("section", "head", seq),
        P("section", "head"),
        P(),
    )
    out_specs = P("section", seq, "head")
    return jax.shard_map(
        on_device, mesh=split_mesh, in_specs=in_specs, out_specs=out_specs, check_vma=False
    )
```

```python
from functools import partial
import math

import jax
import jax.numpy as jnp
from jax import lax
from jax.sharding import Mesh, PartitionSpec as P

HD = 128
SPATIAL = 1


def shifted(block, axis, count, distance, wanted):
    devices = range(count)
    route = [(i - distance, i) for i in devices if i - distance in devices and wanted(i)]
    return lax.ppermute(block, axis, route)


def needs(offset):
    if offset == 3:
        return lambda i: i % 2 == 1
    if offset == -3:
        return lambda i: i % 2 == 0
    return lambda i: True


def linear_pairs(sizes, mapping):
    def flat(index):
        value = 0
        for part, size in zip(index, sizes):
            value = value * size + part
        return value

    grid = [[]]
    for size in sizes:
        grid = [index + [part] for index in grid for part in range(size)]
    return [(flat(index), flat(mapping(*index))) for index in grid]


def from_behind(value, axis, steps):
    count = lax.axis_size(axis)
    pairs = [(source, (source + steps) % count) for source in range(count)]
    return lax.ppermute(value, axis, pairs)


def split_heads(slab, head_count):
    return slab.reshape(slab.shape[0], head_count, slab.shape[1] // head_count)


def tile_maxima(key_slab, head_count, spatial_count):
    parts = split_heads(key_slab, head_count).astype(jnp.float32)
    lengths = jnp.sqrt(jnp.sum(parts * parts, axis=2))
    return jnp.max(lengths.reshape(spatial_count, -1, head_count), axis=1)


def slab_keep(nearby, slab_tile, in_range, spatial_count, temporal_count):
    first = jnp.clip(slab_tile, 0, temporal_count - 1) * spatial_count
    return lax.dynamic_slice_in_dim(nearby, first, spatial_count, 1) & in_range


def attend(
    running,
    slab_entry,
    keep,
    query_parts,
    row_bound,
    head_count,
    spatial_count,
    tile_rows,
    score_scale,
):
    weighted, summed = running
    row_count = query_parts.shape[0]
    slab_keys = split_heads(slab_entry[0], head_count)
    slab_values = split_heads(slab_entry[1], head_count)
    scores = (
        jnp.einsum("qhd,khd->hqk", query_parts, slab_keys, preferred_element_type=jnp.float32)
        * score_scale
    )
    row_keep = jnp.broadcast_to(
        keep[:, None, :, None], (spatial_count, tile_rows, spatial_count, tile_rows)
    )
    row_keep = row_keep.reshape(row_count, row_count)
    weights = jnp.where(row_keep[None], jnp.exp(scores - row_bound.T[:, :, None]), 0.0)
    summed = summed + jnp.sum(weights, axis=2)
    weighted = weighted + jnp.einsum(
        "hqk,khd->qhd",
        weights.astype(jnp.bfloat16),
        slab_values,
        preferred_element_type=jnp.float32,
    )
    return (weighted, summed)


def on_device(query_heads, key_heads, value_heads, stream, out_weight, gate_scale, windows):
    queries = query_heads[0]
    own_keys = key_heads[0]
    own_values = value_heads[0]
    row_count, feature_count = queries.shape
    head_count = feature_count // HD
    spatial_count = SPATIAL
    tile_rows = row_count // spatial_count
    tile_count = windows.shape[0]
    temporal_count = tile_count // spatial_count
    score_scale = 1.0 / math.sqrt(HD)
    x_count = lax.axis_size("sx")
    y_count = lax.axis_size("sy")
    head_groups = lax.axis_size("head")
    sections = lax.axis_size("section")
    seq_count = x_count * y_count
    x_index = lax.axis_index("sx")
    y_index = lax.axis_index("sy")
    position = x_index * y_count + y_index
    parity = position % 2
    temporal = position // 2
    allowed = jnp.any(
        windows[:, :, None] == jnp.arange(tile_count, dtype=jnp.int32)[None, None, :], axis=1
    )
    row_allowed = lax.dynamic_index_in_dim(allowed, temporal, 0, keepdims=False)
    seq = ("sx", "sy")
    half = feature_count // 2
    own_heads = head_count // 2
    tile_len = 2 * row_count
    partner = [(i, i ^ 1) for i in range(seq_count)]

    def partner_half(block):
        return lax.dynamic_slice_in_dim(block, (1 - parity) * half, half, 1)

    def own_half(block):
        return lax.dynamic_slice_in_dim(block, parity * half, half, 1)

    sent = lax.ppermute(
        (partner_half(queries), partner_half(own_keys), partner_half(own_values)), seq, partner
    )

    def whole_tile(mine, theirs):
        return jnp.where(
            parity == 0,
            jnp.concatenate([mine, theirs], axis=0),
            jnp.concatenate([theirs, mine], axis=0),
        )

    tile_q = whole_tile(own_half(queries), sent[0])
    tile_k = whole_tile(own_half(own_keys), sent[1])
    tile_v = whole_tile(own_half(own_values), sent[2])
    before = lax.ppermute((tile_k, tile_v), seq, [(i, i + 2) for i in range(seq_count - 2)])
    after = lax.ppermute((tile_k, tile_v), seq, [(i, i - 2) for i in range(2, seq_count)])
    key_tiles = [before, (tile_k, tile_v), after]
    keeps = []
    for step in (-1, 0, 1):
        near = temporal + step
        in_range = (near >= 0) & (near < temporal_count)
        listed = lax.dynamic_index_in_dim(
            row_allowed, jnp.clip(near, 0, temporal_count - 1), 0, keepdims=False
        )
        keeps.append(in_range & listed)
    bound = jnp.zeros((own_heads,), jnp.float32)
    for (keys, _), keep in zip(key_tiles, keeps):
        key_float = keys.reshape(tile_len, own_heads, HD).astype(jnp.float32)
        key_lengths = jnp.sqrt(jnp.sum(key_float * key_float, axis=2))
        bound = jnp.maximum(bound, jnp.where(keep, jnp.max(key_lengths, axis=0), 0.0))
    query_parts = tile_q.reshape(tile_len, own_heads, HD)
    query_float = query_parts.astype(jnp.float32)
    query_lengths = jnp.sqrt(jnp.sum(query_float * query_float, axis=2))
    row_bound = query_lengths * bound[None, :] * score_scale
    weight_block = lax.all_gather(out_weight[0], "sy", axis=1, tiled=True)
    weight_block, row_bound = lax.optimization_barrier((weight_block, row_bound))
    weighted = jnp.zeros((tile_len, own_heads, HD), jnp.float32)
    summed = jnp.zeros((own_heads, tile_len), jnp.float32)
    for (keys, values), keep in zip(key_tiles, keeps):
        key_parts = keys.reshape(tile_len, own_heads, HD)
        value_parts = values.reshape(tile_len, own_heads, HD)
        scores = (
            jnp.einsum("qhd,khd->hqk", query_parts, key_parts, preferred_element_type=jnp.float32)
            * score_scale
        )
        weights = jnp.where(keep, jnp.exp(scores - row_bound.T[:, :, None]), 0.0)
        summed = summed + jnp.sum(weights, axis=2)
        weighted = weighted + jnp.einsum(
            "hqk,khd->qhd",
            weights.astype(jnp.bfloat16),
            value_parts,
            preferred_element_type=jnp.float32,
        )
    tile_out = (weighted / summed.T[:, :, None]).astype(jnp.bfloat16).reshape(tile_len, half)
    mine_rows = lax.dynamic_slice_in_dim(tile_out, parity * row_count, row_count, 0)
    their_rows = lax.dynamic_slice_in_dim(tile_out, (1 - parity) * row_count, row_count, 0)
    back = lax.ppermute(their_rows, seq, partner)
    attended = jnp.where(
        parity == 0,
        jnp.concatenate([mine_rows, back], axis=1),
        jnp.concatenate([back, mine_rows], axis=1),
    )
    spread = jnp.broadcast_to(attended[None], (x_count,) + attended.shape)
    token_parts = lax.all_to_all(spread, "sx", 0, 0)
    terms = jnp.stack(
        [
            jnp.dot(token_parts[j], weight_block, preferred_element_type=jnp.float32).astype(
                jnp.bfloat16
            )
            for j in range(x_count)
        ]
    )
    split = row_count // 2
    offloaded = lax.psum_scatter(
        terms[:, :split].reshape(head_groups * split, terms.shape[2]),
        "head",
        scatter_dimension=0,
        tiled=True,
    )
    arrived = lax.all_to_all(terms[:, split:], "head", 0, 0)
    mixed = jnp.concatenate(
        [offloaded.astype(jnp.float32), jnp.sum(arrived.astype(jnp.float32), axis=0)], axis=0
    )
    swap = linear_pairs((x_count, head_groups), lambda a, b: (b, a))
    stream_block = lax.ppermute(stream[0], ("sx", "head"), swap)
    gate_block = lax.ppermute(gate_scale[0], ("sx", "head"), swap)
    updated = (stream_block.astype(jnp.float32) + gate_block[None, :] * mixed).astype(jnp.bfloat16)
    hand = linear_pairs(
        (sections, x_count, head_groups), lambda s, a, b: ((s + 1) % sections, b, a)
    )
    handed = lax.ppermute(updated, ("section", "sx", "head"), hand)
    return handed[None]


def solution(mesh):
    sections, seq_count, head_count = mesh.devices.shape
    x_count = 4 if seq_count % 4 == 0 else 1
    split_mesh = Mesh(
        mesh.devices.reshape(sections, x_count, seq_count // x_count, head_count),
        ("section", "sx", "sy", "head"),
    )
    seq = ("sx", "sy")
    in_specs = (
        P("section", seq, "head"),
        P("section", seq, "head"),
        P("section", seq, "head"),
        P("section", seq, "head"),
        P("section", "head", seq),
        P("section", "head"),
        P(),
    )
    out_specs = P("section", seq, "head")
    return jax.shard_map(
        on_device, mesh=split_mesh, in_specs=in_specs, out_specs=out_specs, check_vma=False
    )
```

```python
from functools import partial
import math

import jax
import jax.numpy as jnp
from jax import lax
from jax.sharding import Mesh, PartitionSpec as P

HD = 128
SPATIAL = 1


def shifted(block, axis, count, distance, wanted):
    devices = range(count)
    route = [(i - distance, i) for i in devices if i - distance in devices and wanted(i)]
    return lax.ppermute(block, axis, route)


def needs(offset):
    if offset == 3:
        return lambda i: i % 2 == 1
    if offset == -3:
        return lambda i: i % 2 == 0
    return lambda i: True


def linear_pairs(sizes, mapping):
    def flat(index):
        value = 0
        for part, size in zip(index, sizes):
            value = value * size + part
        return value

    grid = [[]]
    for size in sizes:
        grid = [index + [part] for index in grid for part in range(size)]
    return [(flat(index), flat(mapping(*index))) for index in grid]


def from_behind(value, axis, steps):
    count = lax.axis_size(axis)
    pairs = [(source, (source + steps) % count) for source in range(count)]
    return lax.ppermute(value, axis, pairs)


def split_heads(slab, head_count):
    return slab.reshape(slab.shape[0], head_count, slab.shape[1] // head_count)


def tile_maxima(key_slab, head_count, spatial_count):
    parts = split_heads(key_slab, head_count).astype(jnp.float32)
    lengths = jnp.sqrt(jnp.sum(parts * parts, axis=2))
    return jnp.max(lengths.reshape(spatial_count, -1, head_count), axis=1)


def slab_keep(nearby, slab_tile, in_range, spatial_count, temporal_count):
    first = jnp.clip(slab_tile, 0, temporal_count - 1) * spatial_count
    return lax.dynamic_slice_in_dim(nearby, first, spatial_count, 1) & in_range


def attend(
    running,
    slab_entry,
    keep,
    query_parts,
    row_bound,
    head_count,
    spatial_count,
    tile_rows,
    score_scale,
):
    weighted, summed = running
    row_count = query_parts.shape[0]
    slab_keys = split_heads(slab_entry[0], head_count)
    slab_values = split_heads(slab_entry[1], head_count)
    scores = (
        jnp.einsum("qhd,khd->hqk", query_parts, slab_keys, preferred_element_type=jnp.float32)
        * score_scale
    )
    row_keep = jnp.broadcast_to(
        keep[:, None, :, None], (spatial_count, tile_rows, spatial_count, tile_rows)
    )
    row_keep = row_keep.reshape(row_count, row_count)
    weights = jnp.where(row_keep[None], jnp.exp(scores - row_bound.T[:, :, None]), 0.0)
    summed = summed + jnp.sum(weights, axis=2)
    weighted = weighted + jnp.einsum(
        "hqk,khd->qhd",
        weights.astype(jnp.bfloat16),
        slab_values,
        preferred_element_type=jnp.float32,
    )
    return (weighted, summed)


def on_device(query_heads, key_heads, value_heads, stream, out_weight, gate_scale, windows):
    queries = query_heads[0]
    own_keys = key_heads[0]
    own_values = value_heads[0]
    row_count, feature_count = queries.shape
    head_count = feature_count // HD
    spatial_count = SPATIAL
    tile_rows = row_count // spatial_count
    tile_count = windows.shape[0]
    temporal_count = tile_count // spatial_count
    score_scale = 1.0 / math.sqrt(HD)
    x_count = lax.axis_size("sx")
    y_count = lax.axis_size("sy")
    head_groups = lax.axis_size("head")
    sections = lax.axis_size("section")
    seq_count = x_count * y_count
    x_index = lax.axis_index("sx")
    y_index = lax.axis_index("sy")
    position = x_index * y_count + y_index
    parity = position % 2
    temporal = position // 2
    allowed = jnp.any(
        windows[:, :, None] == jnp.arange(tile_count, dtype=jnp.int32)[None, None, :], axis=1
    )
    row_allowed = lax.dynamic_index_in_dim(allowed, temporal, 0, keepdims=False)
    seq = ("sx", "sy")
    half = feature_count // 2
    own_heads = head_count // 2
    tile_len = 2 * row_count
    partner = [(i, i ^ 1) for i in range(seq_count)]

    def partner_half(block):
        return lax.dynamic_slice_in_dim(block, (1 - parity) * half, half, 1)

    def own_half(block):
        return lax.dynamic_slice_in_dim(block, parity * half, half, 1)

    sent = lax.ppermute(
        (partner_half(queries), partner_half(own_keys), partner_half(own_values)), seq, partner
    )

    def whole_tile(mine, theirs):
        return jnp.where(
            parity == 0,
            jnp.concatenate([mine, theirs], axis=0),
            jnp.concatenate([theirs, mine], axis=0),
        )

    tile_q = whole_tile(own_half(queries), sent[0])
    tile_k = whole_tile(own_half(own_keys), sent[1])
    tile_v = whole_tile(own_half(own_values), sent[2])
    before = lax.ppermute((tile_k, tile_v), seq, [(i, i + 2) for i in range(seq_count - 2)])
    after = lax.ppermute((tile_k, tile_v), seq, [(i, i - 2) for i in range(2, seq_count)])
    key_tiles = [before, (tile_k, tile_v), after]
    keeps = []
    for step in (-1, 0, 1):
        near = temporal + step
        in_range = (near >= 0) & (near < temporal_count)
        listed = lax.dynamic_index_in_dim(
            row_allowed, jnp.clip(near, 0, temporal_count - 1), 0, keepdims=False
        )
        keeps.append(in_range & listed)
    bound = jnp.zeros((own_heads,), jnp.float32)
    for (keys, _), keep in zip(key_tiles, keeps):
        key_float = keys.reshape(tile_len, own_heads, HD).astype(jnp.float32)
        key_lengths = jnp.sqrt(jnp.sum(key_float * key_float, axis=2))
        bound = jnp.maximum(bound, jnp.where(keep, jnp.max(key_lengths, axis=0), 0.0))
    query_parts = tile_q.reshape(tile_len, own_heads, HD)
    query_float = query_parts.astype(jnp.float32)
    query_lengths = jnp.sqrt(jnp.sum(query_float * query_float, axis=2))
    row_bound = query_lengths * bound[None, :] * score_scale
    weight_block = lax.all_gather(out_weight[0], "sy", axis=1, tiled=True)
    weight_block, row_bound = lax.optimization_barrier((weight_block, row_bound))
    weighted = jnp.zeros((tile_len, own_heads, HD), jnp.float32)
    summed = jnp.zeros((own_heads, tile_len), jnp.float32)
    for (keys, values), keep in zip(key_tiles, keeps):
        key_parts = keys.reshape(tile_len, own_heads, HD)
        value_parts = values.reshape(tile_len, own_heads, HD)
        scores = (
            jnp.einsum("qhd,khd->hqk", query_parts, key_parts, preferred_element_type=jnp.float32)
            * score_scale
        )
        weights = jnp.where(keep, jnp.exp(scores - row_bound.T[:, :, None]), 0.0)
        summed = summed + jnp.sum(weights, axis=2)
        weighted = weighted + jnp.einsum(
            "hqk,khd->qhd",
            weights.astype(jnp.bfloat16),
            value_parts,
            preferred_element_type=jnp.float32,
        )
    tile_out = (weighted / summed.T[:, :, None]).astype(jnp.bfloat16).reshape(tile_len, half)
    mine_rows = lax.dynamic_slice_in_dim(tile_out, parity * row_count, row_count, 0)
    their_rows = lax.dynamic_slice_in_dim(tile_out, (1 - parity) * row_count, row_count, 0)
    back = lax.ppermute(their_rows, seq, partner)
    attended = jnp.where(
        parity == 0,
        jnp.concatenate([mine_rows, back], axis=1),
        jnp.concatenate([back, mine_rows], axis=1),
    )
    spread = jnp.broadcast_to(attended[None], (x_count,) + attended.shape)
    token_parts = lax.all_to_all(spread, "sx", 0, 0)
    terms = jnp.stack(
        [
            jnp.dot(token_parts[j], weight_block, preferred_element_type=jnp.float32).astype(
                jnp.bfloat16
            )
            for j in range(x_count)
        ]
    )
    group_index = lax.axis_index("head")
    mixed = lax.dynamic_index_in_dim(terms, group_index, 0, keepdims=False).astype(jnp.float32)
    for shift in range(1, head_groups):
        outgoing = lax.dynamic_index_in_dim(
            terms, (group_index + shift) % head_groups, 0, keepdims=False
        )
        route = [(g, (g + shift) % head_groups) for g in range(head_groups)]
        mixed = mixed + lax.ppermute(outgoing, "head", route).astype(jnp.float32)
    swap = linear_pairs((x_count, head_groups), lambda a, b: (b, a))
    stream_block = lax.ppermute(stream[0], ("sx", "head"), swap)
    gate_block = lax.ppermute(gate_scale[0], ("sx", "head"), swap)
    updated = (stream_block.astype(jnp.float32) + gate_block[None, :] * mixed).astype(jnp.bfloat16)
    hand = linear_pairs(
        (sections, x_count, head_groups), lambda s, a, b: ((s + 1) % sections, b, a)
    )
    handed = lax.ppermute(updated, ("section", "sx", "head"), hand)
    return handed[None]


def solution(mesh):
    sections, seq_count, head_count = mesh.devices.shape
    x_count = 4 if seq_count % 4 == 0 else 1
    split_mesh = Mesh(
        mesh.devices.reshape(sections, x_count, seq_count // x_count, head_count),
        ("section", "sx", "sy", "head"),
    )
    seq = ("sx", "sy")
    in_specs = (
        P("section", seq, "head"),
        P("section", seq, "head"),
        P("section", seq, "head"),
        P("section", seq, "head"),
        P("section", "head", seq),
        P("section", "head"),
        P(),
    )
    out_specs = P("section", seq, "head")
    return jax.shard_map(
        on_device, mesh=split_mesh, in_specs=in_specs, out_specs=out_specs, check_vma=False
    )
```

```python
from functools import partial
import math

import jax
import jax.numpy as jnp
from jax import lax
from jax.sharding import Mesh, PartitionSpec as P

HD = 128
SPATIAL = 1


def shifted(block, axis, count, distance, wanted):
    devices = range(count)
    route = [(i - distance, i) for i in devices if i - distance in devices and wanted(i)]
    return lax.ppermute(block, axis, route)


def needs(offset):
    if offset == 3:
        return lambda i: i % 2 == 1
    if offset == -3:
        return lambda i: i % 2 == 0
    return lambda i: True


def linear_pairs(sizes, mapping):
    def flat(index):
        value = 0
        for part, size in zip(index, sizes):
            value = value * size + part
        return value

    grid = [[]]
    for size in sizes:
        grid = [index + [part] for index in grid for part in range(size)]
    return [(flat(index), flat(mapping(*index))) for index in grid]


def from_behind(value, axis, steps):
    count = lax.axis_size(axis)
    pairs = [(source, (source + steps) % count) for source in range(count)]
    return lax.ppermute(value, axis, pairs)


def split_heads(slab, head_count):
    return slab.reshape(slab.shape[0], head_count, slab.shape[1] // head_count)


def tile_maxima(key_slab, head_count, spatial_count):
    parts = split_heads(key_slab, head_count).astype(jnp.float32)
    lengths = jnp.sqrt(jnp.sum(parts * parts, axis=2))
    return jnp.max(lengths.reshape(spatial_count, -1, head_count), axis=1)


def slab_keep(nearby, slab_tile, in_range, spatial_count, temporal_count):
    first = jnp.clip(slab_tile, 0, temporal_count - 1) * spatial_count
    return lax.dynamic_slice_in_dim(nearby, first, spatial_count, 1) & in_range


def attend(
    running,
    slab_entry,
    keep,
    query_parts,
    row_bound,
    head_count,
    spatial_count,
    tile_rows,
    score_scale,
):
    weighted, summed = running
    row_count = query_parts.shape[0]
    slab_keys = split_heads(slab_entry[0], head_count)
    slab_values = split_heads(slab_entry[1], head_count)
    scores = (
        jnp.einsum("qhd,khd->hqk", query_parts, slab_keys, preferred_element_type=jnp.float32)
        * score_scale
    )
    row_keep = jnp.broadcast_to(
        keep[:, None, :, None], (spatial_count, tile_rows, spatial_count, tile_rows)
    )
    row_keep = row_keep.reshape(row_count, row_count)
    weights = jnp.where(row_keep[None], jnp.exp(scores - row_bound.T[:, :, None]), 0.0)
    summed = summed + jnp.sum(weights, axis=2)
    weighted = weighted + jnp.einsum(
        "hqk,khd->qhd",
        weights.astype(jnp.bfloat16),
        slab_values,
        preferred_element_type=jnp.float32,
    )
    return (weighted, summed)


def on_device(query_heads, key_heads, value_heads, stream, out_weight, gate_scale, windows):
    queries = query_heads[0]
    own_keys = key_heads[0]
    own_values = value_heads[0]
    row_count, feature_count = queries.shape
    head_count = feature_count // HD
    spatial_count = SPATIAL
    tile_rows = row_count // spatial_count
    tile_count = windows.shape[0]
    temporal_count = tile_count // spatial_count
    score_scale = 1.0 / math.sqrt(HD)
    x_count = lax.axis_size("sx")
    y_count = lax.axis_size("sy")
    head_groups = lax.axis_size("head")
    sections = lax.axis_size("section")
    seq_count = x_count * y_count
    x_index = lax.axis_index("sx")
    y_index = lax.axis_index("sy")
    position = x_index * y_count + y_index
    parity = position % 2
    temporal = position // 2
    allowed = jnp.any(
        windows[:, :, None] == jnp.arange(tile_count, dtype=jnp.int32)[None, None, :], axis=1
    )
    row_allowed = lax.dynamic_index_in_dim(allowed, temporal, 0, keepdims=False)
    seq = ("sx", "sy")
    half = feature_count // 2
    own_heads = head_count // 2
    tile_len = 2 * row_count
    partner = [(i, i ^ 1) for i in range(seq_count)]

    def partner_half(block):
        return lax.dynamic_slice_in_dim(block, (1 - parity) * half, half, 1)

    def own_half(block):
        return lax.dynamic_slice_in_dim(block, parity * half, half, 1)

    sent = lax.ppermute(
        (partner_half(queries), partner_half(own_keys), partner_half(own_values)), seq, partner
    )

    def whole_tile(mine, theirs):
        return jnp.where(
            parity == 0,
            jnp.concatenate([mine, theirs], axis=0),
            jnp.concatenate([theirs, mine], axis=0),
        )

    tile_q = whole_tile(own_half(queries), sent[0])
    tile_k = whole_tile(own_half(own_keys), sent[1])
    tile_v = whole_tile(own_half(own_values), sent[2])
    before = lax.ppermute((tile_k, tile_v), seq, [(i, i + 2) for i in range(seq_count - 2)])
    after = lax.ppermute((tile_k, tile_v), seq, [(i, i - 2) for i in range(2, seq_count)])
    key_tiles = [before, (tile_k, tile_v), after]
    keeps = []
    for step in (-1, 0, 1):
        near = temporal + step
        in_range = (near >= 0) & (near < temporal_count)
        listed = lax.dynamic_index_in_dim(
            row_allowed, jnp.clip(near, 0, temporal_count - 1), 0, keepdims=False
        )
        keeps.append(in_range & listed)
    bound = jnp.zeros((own_heads,), jnp.float32)
    for (keys, _), keep in zip(key_tiles, keeps):
        key_float = keys.reshape(tile_len, own_heads, HD).astype(jnp.float32)
        key_lengths = jnp.sqrt(jnp.sum(key_float * key_float, axis=2))
        bound = jnp.maximum(bound, jnp.where(keep, jnp.max(key_lengths, axis=0), 0.0))
    query_parts = tile_q.reshape(tile_len, own_heads, HD)
    query_float = query_parts.astype(jnp.float32)
    query_lengths = jnp.sqrt(jnp.sum(query_float * query_float, axis=2))
    row_bound = query_lengths * bound[None, :] * score_scale
    weight_block = lax.all_gather(out_weight[0], "sy", axis=1, tiled=True)
    weight_block, row_bound = lax.optimization_barrier((weight_block, row_bound))
    weighted = jnp.zeros((tile_len, own_heads, HD), jnp.float32)
    summed = jnp.zeros((own_heads, tile_len), jnp.float32)
    for (keys, values), keep in zip(key_tiles, keeps):
        key_parts = keys.reshape(tile_len, own_heads, HD)
        value_parts = values.reshape(tile_len, own_heads, HD)
        scores = (
            jnp.einsum("qhd,khd->hqk", query_parts, key_parts, preferred_element_type=jnp.float32)
            * score_scale
        )
        weights = jnp.where(keep, jnp.exp(scores - row_bound.T[:, :, None]), 0.0)
        summed = summed + jnp.sum(weights, axis=2)
        weighted = weighted + jnp.einsum(
            "hqk,khd->qhd",
            weights.astype(jnp.bfloat16),
            value_parts,
            preferred_element_type=jnp.float32,
        )
    tile_out = (weighted / summed.T[:, :, None]).astype(jnp.bfloat16).reshape(tile_len, half)
    mine_rows = lax.dynamic_slice_in_dim(tile_out, parity * row_count, row_count, 0)
    their_rows = lax.dynamic_slice_in_dim(tile_out, (1 - parity) * row_count, row_count, 0)
    back = lax.ppermute(their_rows, seq, partner)
    attended = jnp.where(
        parity == 0,
        jnp.concatenate([mine_rows, back], axis=1),
        jnp.concatenate([back, mine_rows], axis=1),
    )
    token_parts = [attended] + [
        lax.ppermute(attended, "sx", [(i, (i + d) % x_count) for i in range(x_count)])
        for d in range(1, x_count)
    ]
    terms = jnp.stack(
        [
            jnp.dot(part, weight_block, preferred_element_type=jnp.float32).astype(jnp.bfloat16)
            for part in token_parts
        ]
    )

    def term_for(slab_x):
        return lax.dynamic_index_in_dim(terms, (x_index - slab_x) % x_count, 0, keepdims=False)

    group_index = lax.axis_index("head")
    mixed = term_for(group_index).astype(jnp.float32)
    for shift in range(1, head_groups):
        outgoing = term_for((group_index + shift) % head_groups)
        route = [(g, (g + shift) % head_groups) for g in range(head_groups)]
        mixed = mixed + lax.ppermute(outgoing, "head", route).astype(jnp.float32)
    swap = linear_pairs((x_count, head_groups), lambda a, b: (b, a))
    stream_block = lax.ppermute(stream[0], ("sx", "head"), swap)
    gate_block = lax.ppermute(gate_scale[0], ("sx", "head"), swap)
    updated = (stream_block.astype(jnp.float32) + gate_block[None, :] * mixed).astype(jnp.bfloat16)
    hand = linear_pairs(
        (sections, x_count, head_groups), lambda s, a, b: ((s + 1) % sections, b, a)
    )
    handed = lax.ppermute(updated, ("section", "sx", "head"), hand)
    return handed[None]


def solution(mesh):
    sections, seq_count, head_count = mesh.devices.shape
    x_count = 4 if seq_count % 4 == 0 else 1
    split_mesh = Mesh(
        mesh.devices.reshape(sections, x_count, seq_count // x_count, head_count),
        ("section", "sx", "sy", "head"),
    )
    seq = ("sx", "sy")
    in_specs = (
        P("section", seq, "head"),
        P("section", seq, "head"),
        P("section", seq, "head"),
        P("section", seq, "head"),
        P("section", "head", seq),
        P("section", "head"),
        P(),
    )
    out_specs = P("section", seq, "head")
    return jax.shard_map(
        on_device, mesh=split_mesh, in_specs=in_specs, out_specs=out_specs, check_vma=False
    )
```

```python
from functools import partial
import math

import jax
import jax.numpy as jnp
from jax import lax
from jax.sharding import Mesh, PartitionSpec as P

HD = 128
SPATIAL = 1


def shifted(block, axis, count, distance, wanted):
    devices = range(count)
    route = [(i - distance, i) for i in devices if i - distance in devices and wanted(i)]
    return lax.ppermute(block, axis, route)


def needs(offset):
    if offset == 3:
        return lambda i: i % 2 == 1
    if offset == -3:
        return lambda i: i % 2 == 0
    return lambda i: True


def linear_pairs(sizes, mapping):
    def flat(index):
        value = 0
        for part, size in zip(index, sizes):
            value = value * size + part
        return value

    grid = [[]]
    for size in sizes:
        grid = [index + [part] for index in grid for part in range(size)]
    return [(flat(index), flat(mapping(*index))) for index in grid]


def from_behind(value, axis, steps):
    count = lax.axis_size(axis)
    pairs = [(source, (source + steps) % count) for source in range(count)]
    return lax.ppermute(value, axis, pairs)


def split_heads(slab, head_count):
    return slab.reshape(slab.shape[0], head_count, slab.shape[1] // head_count)


def tile_maxima(key_slab, head_count, spatial_count):
    parts = split_heads(key_slab, head_count).astype(jnp.float32)
    lengths = jnp.sqrt(jnp.sum(parts * parts, axis=2))
    return jnp.max(lengths.reshape(spatial_count, -1, head_count), axis=1)


def slab_keep(nearby, slab_tile, in_range, spatial_count, temporal_count):
    first = jnp.clip(slab_tile, 0, temporal_count - 1) * spatial_count
    return lax.dynamic_slice_in_dim(nearby, first, spatial_count, 1) & in_range


def attend(
    running,
    slab_entry,
    keep,
    query_parts,
    row_bound,
    head_count,
    spatial_count,
    tile_rows,
    score_scale,
):
    weighted, summed = running
    row_count = query_parts.shape[0]
    slab_keys = split_heads(slab_entry[0], head_count)
    slab_values = split_heads(slab_entry[1], head_count)
    scores = (
        jnp.einsum("qhd,khd->hqk", query_parts, slab_keys, preferred_element_type=jnp.float32)
        * score_scale
    )
    row_keep = jnp.broadcast_to(
        keep[:, None, :, None], (spatial_count, tile_rows, spatial_count, tile_rows)
    )
    row_keep = row_keep.reshape(row_count, row_count)
    weights = jnp.where(row_keep[None], jnp.exp(scores - row_bound.T[:, :, None]), 0.0)
    summed = summed + jnp.sum(weights, axis=2)
    weighted = weighted + jnp.einsum(
        "hqk,khd->qhd",
        weights.astype(jnp.bfloat16),
        slab_values,
        preferred_element_type=jnp.float32,
    )
    return (weighted, summed)


def on_device(query_heads, key_heads, value_heads, stream, out_weight, gate_scale, windows):
    queries = query_heads[0]
    own_keys = key_heads[0]
    own_values = value_heads[0]
    row_count, feature_count = queries.shape
    head_count = feature_count // HD
    spatial_count = SPATIAL
    tile_rows = row_count // spatial_count
    tile_count = windows.shape[0]
    temporal_count = tile_count // spatial_count
    score_scale = 1.0 / math.sqrt(HD)
    x_count = lax.axis_size("sx")
    y_count = lax.axis_size("sy")
    head_groups = lax.axis_size("head")
    sections = lax.axis_size("section")
    seq_count = x_count * y_count
    x_index = lax.axis_index("sx")
    y_index = lax.axis_index("sy")
    position = x_index * y_count + y_index
    parity = position % 2
    temporal = position // 2
    allowed = jnp.any(
        windows[:, :, None] == jnp.arange(tile_count, dtype=jnp.int32)[None, None, :], axis=1
    )
    row_allowed = lax.dynamic_index_in_dim(allowed, temporal, 0, keepdims=False)
    seq = ("sx", "sy")
    half = feature_count // 2
    own_heads = head_count // 2
    tile_len = 2 * row_count
    partner = [(i, i ^ 1) for i in range(seq_count)]

    def partner_half(block):
        return lax.dynamic_slice_in_dim(block, (1 - parity) * half, half, 1)

    def own_half(block):
        return lax.dynamic_slice_in_dim(block, parity * half, half, 1)

    sent = lax.ppermute(
        (partner_half(queries), partner_half(own_keys), partner_half(own_values)), seq, partner
    )

    def whole_tile(mine, theirs):
        return jnp.where(
            parity == 0,
            jnp.concatenate([mine, theirs], axis=0),
            jnp.concatenate([theirs, mine], axis=0),
        )

    tile_q = whole_tile(own_half(queries), sent[0])
    tile_k = whole_tile(own_half(own_keys), sent[1])
    tile_v = whole_tile(own_half(own_values), sent[2])
    before = lax.ppermute((tile_k, tile_v), seq, [(i, i + 2) for i in range(seq_count - 2)])
    after = lax.ppermute((tile_k, tile_v), seq, [(i, i - 2) for i in range(2, seq_count)])
    key_tiles = [before, (tile_k, tile_v), after]
    keeps = []
    for step in (-1, 0, 1):
        near = temporal + step
        in_range = (near >= 0) & (near < temporal_count)
        listed = lax.dynamic_index_in_dim(
            row_allowed, jnp.clip(near, 0, temporal_count - 1), 0, keepdims=False
        )
        keeps.append(in_range & listed)
    bound = jnp.zeros((own_heads,), jnp.float32)
    for (keys, _), keep in zip(key_tiles, keeps):
        key_float = keys.reshape(tile_len, own_heads, HD).astype(jnp.float32)
        key_lengths = jnp.sqrt(jnp.sum(key_float * key_float, axis=2))
        bound = jnp.maximum(bound, jnp.where(keep, jnp.max(key_lengths, axis=0), 0.0))
    query_parts = tile_q.reshape(tile_len, own_heads, HD)
    query_float = query_parts.astype(jnp.float32)
    query_lengths = jnp.sqrt(jnp.sum(query_float * query_float, axis=2))
    row_bound = query_lengths * bound[None, :] * score_scale
    weight_block = lax.all_gather(out_weight[0], "sy", axis=1, tiled=True)
    swap = linear_pairs((x_count, head_groups), lambda a, b: (b, a))
    stream_block = lax.ppermute(stream[0], ("sx", "head"), swap)
    gate_block = lax.ppermute(gate_scale[0], ("sx", "head"), swap)
    weight_block, row_bound, stream_block, gate_block = lax.optimization_barrier(
        (weight_block, row_bound, stream_block, gate_block)
    )
    weighted = jnp.zeros((tile_len, own_heads, HD), jnp.float32)
    summed = jnp.zeros((own_heads, tile_len), jnp.float32)
    for (keys, values), keep in zip(key_tiles, keeps):
        key_parts = keys.reshape(tile_len, own_heads, HD)
        value_parts = values.reshape(tile_len, own_heads, HD)
        scores = (
            jnp.einsum("qhd,khd->hqk", query_parts, key_parts, preferred_element_type=jnp.float32)
            * score_scale
        )
        weights = jnp.where(keep, jnp.exp(scores - row_bound.T[:, :, None]), 0.0)
        summed = summed + jnp.sum(weights, axis=2)
        weighted = weighted + jnp.einsum(
            "hqk,khd->qhd",
            weights.astype(jnp.bfloat16),
            value_parts,
            preferred_element_type=jnp.float32,
        )
    tile_out = (weighted / summed.T[:, :, None]).astype(jnp.bfloat16).reshape(tile_len, half)
    mine_rows = lax.dynamic_slice_in_dim(tile_out, parity * row_count, row_count, 0)
    their_rows = lax.dynamic_slice_in_dim(tile_out, (1 - parity) * row_count, row_count, 0)
    back = lax.ppermute(their_rows, seq, partner)
    attended = jnp.where(
        parity == 0,
        jnp.concatenate([mine_rows, back], axis=1),
        jnp.concatenate([back, mine_rows], axis=1),
    )
    spread = jnp.broadcast_to(attended[None], (x_count,) + attended.shape)
    token_parts = lax.all_to_all(spread, "sx", 0, 0)
    terms = jnp.stack(
        [
            jnp.dot(token_parts[j], weight_block, preferred_element_type=jnp.float32).astype(
                jnp.bfloat16
            )
            for j in range(x_count)
        ]
    )
    group_index = lax.axis_index("head")
    mixed = lax.dynamic_index_in_dim(terms, group_index, 0, keepdims=False).astype(jnp.float32)
    for shift in range(1, head_groups):
        outgoing = lax.dynamic_index_in_dim(
            terms, (group_index + shift) % head_groups, 0, keepdims=False
        )
        route = [(g, (g + shift) % head_groups) for g in range(head_groups)]
        mixed = mixed + lax.ppermute(outgoing, "head", route).astype(jnp.float32)
    updated = (stream_block.astype(jnp.float32) + gate_block[None, :] * mixed).astype(jnp.bfloat16)
    hand = linear_pairs(
        (sections, x_count, head_groups), lambda s, a, b: ((s + 1) % sections, b, a)
    )
    handed = lax.ppermute(updated, ("section", "sx", "head"), hand)
    return handed[None]


def solution(mesh):
    sections, seq_count, head_count = mesh.devices.shape
    x_count = 4 if seq_count % 4 == 0 else 1
    split_mesh = Mesh(
        mesh.devices.reshape(sections, x_count, seq_count // x_count, head_count),
        ("section", "sx", "sy", "head"),
    )
    seq = ("sx", "sy")
    in_specs = (
        P("section", seq, "head"),
        P("section", seq, "head"),
        P("section", seq, "head"),
        P("section", seq, "head"),
        P("section", "head", seq),
        P("section", "head"),
        P(),
    )
    out_specs = P("section", seq, "head")
    return jax.shard_map(
        on_device, mesh=split_mesh, in_specs=in_specs, out_specs=out_specs, check_vma=False
    )
```

```python
from functools import partial
import math

import jax
import jax.numpy as jnp
from jax import lax
from jax.sharding import Mesh, PartitionSpec as P

HD = 128
SPATIAL = 1


def shifted(block, axis, count, distance, wanted):
    devices = range(count)
    route = [(i - distance, i) for i in devices if i - distance in devices and wanted(i)]
    return lax.ppermute(block, axis, route)


def needs(offset):
    if offset == 3:
        return lambda i: i % 2 == 1
    if offset == -3:
        return lambda i: i % 2 == 0
    return lambda i: True


def linear_pairs(sizes, mapping):
    def flat(index):
        value = 0
        for part, size in zip(index, sizes):
            value = value * size + part
        return value

    grid = [[]]
    for size in sizes:
        grid = [index + [part] for index in grid for part in range(size)]
    return [(flat(index), flat(mapping(*index))) for index in grid]


def from_behind(value, axis, steps):
    count = lax.axis_size(axis)
    pairs = [(source, (source + steps) % count) for source in range(count)]
    return lax.ppermute(value, axis, pairs)


def split_heads(slab, head_count):
    return slab.reshape(slab.shape[0], head_count, slab.shape[1] // head_count)


def tile_maxima(key_slab, head_count, spatial_count):
    parts = split_heads(key_slab, head_count).astype(jnp.float32)
    lengths = jnp.sqrt(jnp.sum(parts * parts, axis=2))
    return jnp.max(lengths.reshape(spatial_count, -1, head_count), axis=1)


def slab_keep(nearby, slab_tile, in_range, spatial_count, temporal_count):
    first = jnp.clip(slab_tile, 0, temporal_count - 1) * spatial_count
    return lax.dynamic_slice_in_dim(nearby, first, spatial_count, 1) & in_range


def attend(
    running,
    slab_entry,
    keep,
    query_parts,
    row_bound,
    head_count,
    spatial_count,
    tile_rows,
    score_scale,
):
    weighted, summed = running
    row_count = query_parts.shape[0]
    slab_keys = split_heads(slab_entry[0], head_count)
    slab_values = split_heads(slab_entry[1], head_count)
    scores = (
        jnp.einsum("qhd,khd->hqk", query_parts, slab_keys, preferred_element_type=jnp.float32)
        * score_scale
    )
    row_keep = jnp.broadcast_to(
        keep[:, None, :, None], (spatial_count, tile_rows, spatial_count, tile_rows)
    )
    row_keep = row_keep.reshape(row_count, row_count)
    weights = jnp.where(row_keep[None], jnp.exp(scores - row_bound.T[:, :, None]), 0.0)
    summed = summed + jnp.sum(weights, axis=2)
    weighted = weighted + jnp.einsum(
        "hqk,khd->qhd",
        weights.astype(jnp.bfloat16),
        slab_values,
        preferred_element_type=jnp.float32,
    )
    return (weighted, summed)


def on_device(query_heads, key_heads, value_heads, stream, out_weight, gate_scale, windows):
    queries = query_heads[0]
    own_keys = key_heads[0]
    own_values = value_heads[0]
    row_count, feature_count = queries.shape
    head_count = feature_count // HD
    spatial_count = SPATIAL
    tile_rows = row_count // spatial_count
    tile_count = windows.shape[0]
    temporal_count = tile_count // spatial_count
    score_scale = 1.0 / math.sqrt(HD)
    x_count = lax.axis_size("sx")
    y_count = lax.axis_size("sy")
    head_groups = lax.axis_size("head")
    sections = lax.axis_size("section")
    seq_count = x_count * y_count
    x_index = lax.axis_index("sx")
    y_index = lax.axis_index("sy")
    position = x_index * y_count + y_index
    parity = position % 2
    temporal = position // 2
    allowed = jnp.any(
        windows[:, :, None] == jnp.arange(tile_count, dtype=jnp.int32)[None, None, :], axis=1
    )
    row_allowed = lax.dynamic_index_in_dim(allowed, temporal, 0, keepdims=False)
    seq = ("sx", "sy")
    half = feature_count // 2
    own_heads = head_count // 2
    tile_len = 2 * row_count
    partner = [(i, i ^ 1) for i in range(seq_count)]

    def partner_half(block):
        return lax.dynamic_slice_in_dim(block, (1 - parity) * half, half, 1)

    def own_half(block):
        return lax.dynamic_slice_in_dim(block, parity * half, half, 1)

    sent = lax.ppermute(
        (partner_half(queries), partner_half(own_keys), partner_half(own_values)), seq, partner
    )

    def whole_tile(mine, theirs):
        return jnp.where(
            parity == 0,
            jnp.concatenate([mine, theirs], axis=0),
            jnp.concatenate([theirs, mine], axis=0),
        )

    tile_q = whole_tile(own_half(queries), sent[0])
    tile_k = whole_tile(own_half(own_keys), sent[1])
    tile_v = whole_tile(own_half(own_values), sent[2])
    before = lax.ppermute((tile_k, tile_v), seq, [(i, i + 2) for i in range(seq_count - 2)])
    after = lax.ppermute((tile_k, tile_v), seq, [(i, i - 2) for i in range(2, seq_count)])
    key_tiles = [before, (tile_k, tile_v), after]
    keeps = []
    for step in (-1, 0, 1):
        near = temporal + step
        in_range = (near >= 0) & (near < temporal_count)
        listed = lax.dynamic_index_in_dim(
            row_allowed, jnp.clip(near, 0, temporal_count - 1), 0, keepdims=False
        )
        keeps.append(in_range & listed)
    bound = jnp.zeros((own_heads,), jnp.float32)
    for (keys, _), keep in zip(key_tiles, keeps):
        key_float = keys.reshape(tile_len, own_heads, HD).astype(jnp.float32)
        key_lengths = jnp.sqrt(jnp.sum(key_float * key_float, axis=2))
        bound = jnp.maximum(bound, jnp.where(keep, jnp.max(key_lengths, axis=0), 0.0))
    query_parts = tile_q.reshape(tile_len, own_heads, HD)
    query_float = query_parts.astype(jnp.float32)
    query_lengths = jnp.sqrt(jnp.sum(query_float * query_float, axis=2))
    row_bound = query_lengths * bound[None, :] * score_scale
    weight_block = lax.all_gather(out_weight[0], "sy", axis=1, tiled=True)
    swap = linear_pairs((x_count, head_groups), lambda a, b: (b, a))
    stream_in, gate_in, _ = lax.optimization_barrier((stream[0], gate_scale[0], tile_k))
    stream_block = lax.ppermute(stream_in, ("sx", "head"), swap)
    gate_block = lax.ppermute(gate_in, ("sx", "head"), swap)
    weight_block, row_bound, stream_block, gate_block = lax.optimization_barrier(
        (weight_block, row_bound, stream_block, gate_block)
    )
    weighted = jnp.zeros((tile_len, own_heads, HD), jnp.float32)
    summed = jnp.zeros((own_heads, tile_len), jnp.float32)
    for (keys, values), keep in zip(key_tiles, keeps):
        key_parts = keys.reshape(tile_len, own_heads, HD)
        value_parts = values.reshape(tile_len, own_heads, HD)
        scores = (
            jnp.einsum("qhd,khd->hqk", query_parts, key_parts, preferred_element_type=jnp.float32)
            * score_scale
        )
        weights = jnp.where(keep, jnp.exp(scores - row_bound.T[:, :, None]), 0.0)
        summed = summed + jnp.sum(weights, axis=2)
        weighted = weighted + jnp.einsum(
            "hqk,khd->qhd",
            weights.astype(jnp.bfloat16),
            value_parts,
            preferred_element_type=jnp.float32,
        )
    tile_out = (weighted / summed.T[:, :, None]).astype(jnp.bfloat16).reshape(tile_len, half)
    mine_rows = lax.dynamic_slice_in_dim(tile_out, parity * row_count, row_count, 0)
    their_rows = lax.dynamic_slice_in_dim(tile_out, (1 - parity) * row_count, row_count, 0)
    back = lax.ppermute(their_rows, seq, partner)
    attended = jnp.where(
        parity == 0,
        jnp.concatenate([mine_rows, back], axis=1),
        jnp.concatenate([back, mine_rows], axis=1),
    )
    spread = jnp.broadcast_to(attended[None], (x_count,) + attended.shape)
    token_parts = lax.all_to_all(spread, "sx", 0, 0)
    terms = jnp.stack(
        [
            jnp.dot(token_parts[j], weight_block, preferred_element_type=jnp.float32).astype(
                jnp.bfloat16
            )
            for j in range(x_count)
        ]
    )
    group_index = lax.axis_index("head")
    mixed = lax.dynamic_index_in_dim(terms, group_index, 0, keepdims=False).astype(jnp.float32)
    for shift in range(1, head_groups):
        outgoing = lax.dynamic_index_in_dim(
            terms, (group_index + shift) % head_groups, 0, keepdims=False
        )
        route = [(g, (g + shift) % head_groups) for g in range(head_groups)]
        mixed = mixed + lax.ppermute(outgoing, "head", route).astype(jnp.float32)
    updated = (stream_block.astype(jnp.float32) + gate_block[None, :] * mixed).astype(jnp.bfloat16)
    hand = linear_pairs(
        (sections, x_count, head_groups), lambda s, a, b: ((s + 1) % sections, b, a)
    )
    handed = lax.ppermute(updated, ("section", "sx", "head"), hand)
    return handed[None]


def solution(mesh):
    sections, seq_count, head_count = mesh.devices.shape
    x_count = 4 if seq_count % 4 == 0 else 1
    split_mesh = Mesh(
        mesh.devices.reshape(sections, x_count, seq_count // x_count, head_count),
        ("section", "sx", "sy", "head"),
    )
    seq = ("sx", "sy")
    in_specs = (
        P("section", seq, "head"),
        P("section", seq, "head"),
        P("section", seq, "head"),
        P("section", seq, "head"),
        P("section", "head", seq),
        P("section", "head"),
        P(),
    )
    out_specs = P("section", seq, "head")
    return jax.shard_map(
        on_device, mesh=split_mesh, in_specs=in_specs, out_specs=out_specs, check_vma=False
    )
```

```python
from functools import partial
import math

import jax
import jax.numpy as jnp
from jax import lax
from jax.sharding import Mesh, PartitionSpec as P

HD = 128
SPATIAL = 1


def shifted(block, axis, count, distance, wanted):
    devices = range(count)
    route = [(i - distance, i) for i in devices if i - distance in devices and wanted(i)]
    return lax.ppermute(block, axis, route)


def needs(offset):
    if offset == 3:
        return lambda i: i % 2 == 1
    if offset == -3:
        return lambda i: i % 2 == 0
    return lambda i: True


def linear_pairs(sizes, mapping):
    def flat(index):
        value = 0
        for part, size in zip(index, sizes):
            value = value * size + part
        return value

    grid = [[]]
    for size in sizes:
        grid = [index + [part] for index in grid for part in range(size)]
    return [(flat(index), flat(mapping(*index))) for index in grid]


def from_behind(value, axis, steps):
    count = lax.axis_size(axis)
    pairs = [(source, (source + steps) % count) for source in range(count)]
    return lax.ppermute(value, axis, pairs)


def split_heads(slab, head_count):
    return slab.reshape(slab.shape[0], head_count, slab.shape[1] // head_count)


def tile_maxima(key_slab, head_count, spatial_count):
    parts = split_heads(key_slab, head_count).astype(jnp.float32)
    lengths = jnp.sqrt(jnp.sum(parts * parts, axis=2))
    return jnp.max(lengths.reshape(spatial_count, -1, head_count), axis=1)


def slab_keep(nearby, slab_tile, in_range, spatial_count, temporal_count):
    first = jnp.clip(slab_tile, 0, temporal_count - 1) * spatial_count
    return lax.dynamic_slice_in_dim(nearby, first, spatial_count, 1) & in_range


def attend(
    running,
    slab_entry,
    keep,
    query_parts,
    row_bound,
    head_count,
    spatial_count,
    tile_rows,
    score_scale,
):
    weighted, summed = running
    row_count = query_parts.shape[0]
    slab_keys = split_heads(slab_entry[0], head_count)
    slab_values = split_heads(slab_entry[1], head_count)
    scores = (
        jnp.einsum("qhd,khd->hqk", query_parts, slab_keys, preferred_element_type=jnp.float32)
        * score_scale
    )
    row_keep = jnp.broadcast_to(
        keep[:, None, :, None], (spatial_count, tile_rows, spatial_count, tile_rows)
    )
    row_keep = row_keep.reshape(row_count, row_count)
    weights = jnp.where(row_keep[None], jnp.exp(scores - row_bound.T[:, :, None]), 0.0)
    summed = summed + jnp.sum(weights, axis=2)
    weighted = weighted + jnp.einsum(
        "hqk,khd->qhd",
        weights.astype(jnp.bfloat16),
        slab_values,
        preferred_element_type=jnp.float32,
    )
    return (weighted, summed)


def on_device(query_heads, key_heads, value_heads, stream, out_weight, gate_scale, windows):
    queries = query_heads[0]
    own_keys = key_heads[0]
    own_values = value_heads[0]
    row_count, feature_count = queries.shape
    head_count = feature_count // HD
    spatial_count = SPATIAL
    tile_rows = row_count // spatial_count
    tile_count = windows.shape[0]
    temporal_count = tile_count // spatial_count
    score_scale = 1.0 / math.sqrt(HD)
    x_count = lax.axis_size("sx")
    y_count = lax.axis_size("sy")
    head_groups = lax.axis_size("head")
    sections = lax.axis_size("section")
    seq_count = x_count * y_count
    x_index = lax.axis_index("sx")
    y_index = lax.axis_index("sy")
    position = x_index * y_count + y_index
    parity = position % 2
    temporal = position // 2
    allowed = jnp.any(
        windows[:, :, None] == jnp.arange(tile_count, dtype=jnp.int32)[None, None, :], axis=1
    )
    row_allowed = lax.dynamic_index_in_dim(allowed, temporal, 0, keepdims=False)
    seq = ("sx", "sy")
    half = feature_count // 2
    own_heads = head_count // 2
    tile_len = 2 * row_count
    partner = [(i, i ^ 1) for i in range(seq_count)]

    def partner_half(block):
        return lax.dynamic_slice_in_dim(block, (1 - parity) * half, half, 1)

    def own_half(block):
        return lax.dynamic_slice_in_dim(block, parity * half, half, 1)

    swapped = lax.ppermute(
        jnp.concatenate(
            [partner_half(queries), partner_half(own_keys), partner_half(own_values)], axis=1
        ),
        seq,
        partner,
    )
    sent = [swapped[:, part * half:(part + 1) * half] for part in range(3)]

    def whole_tile(mine, theirs):
        return jnp.where(
            parity == 0,
            jnp.concatenate([mine, theirs], axis=0),
            jnp.concatenate([theirs, mine], axis=0),
        )

    tile_q = whole_tile(own_half(queries), sent[0])
    tile_k = whole_tile(own_half(own_keys), sent[1])
    tile_v = whole_tile(own_half(own_values), sent[2])
    tile_kv = jnp.concatenate([tile_k, tile_v], axis=1)
    moved = [
        lax.ppermute(tile_kv, seq, [(i, i + 2) for i in range(seq_count - 2)]),
        lax.ppermute(tile_kv, seq, [(i, i - 2) for i in range(2, seq_count)]),
    ]
    before, after = [(block[:, :half], block[:, half:]) for block in moved]
    key_tiles = [before, (tile_k, tile_v), after]
    keeps = []
    for step in (-1, 0, 1):
        near = temporal + step
        in_range = (near >= 0) & (near < temporal_count)
        listed = lax.dynamic_index_in_dim(
            row_allowed, jnp.clip(near, 0, temporal_count - 1), 0, keepdims=False
        )
        keeps.append(in_range & listed)
    bound = jnp.zeros((own_heads,), jnp.float32)
    for (keys, _), keep in zip(key_tiles, keeps):
        key_float = keys.reshape(tile_len, own_heads, HD).astype(jnp.float32)
        key_lengths = jnp.sqrt(jnp.sum(key_float * key_float, axis=2))
        bound = jnp.maximum(bound, jnp.where(keep, jnp.max(key_lengths, axis=0), 0.0))
    query_parts = tile_q.reshape(tile_len, own_heads, HD)
    query_float = query_parts.astype(jnp.float32)
    query_lengths = jnp.sqrt(jnp.sum(query_float * query_float, axis=2))
    row_bound = query_lengths * bound[None, :] * score_scale
    weight_block = lax.all_gather(out_weight[0], "sy", axis=1, tiled=True)
    swap = linear_pairs((x_count, head_groups), lambda a, b: (b, a))
    stream_in, gate_in, _ = lax.optimization_barrier((stream[0], gate_scale[0], tile_k))
    stream_block = lax.ppermute(stream_in, ("sx", "head"), swap)
    gate_block = lax.ppermute(gate_in, ("sx", "head"), swap)
    weight_block, row_bound, stream_block, gate_block = lax.optimization_barrier(
        (weight_block, row_bound, stream_block, gate_block)
    )
    weighted = jnp.zeros((tile_len, own_heads, HD), jnp.float32)
    summed = jnp.zeros((own_heads, tile_len), jnp.float32)
    for (keys, values), keep in zip(key_tiles, keeps):
        key_parts = keys.reshape(tile_len, own_heads, HD)
        value_parts = values.reshape(tile_len, own_heads, HD)
        scores = (
            jnp.einsum("qhd,khd->hqk", query_parts, key_parts, preferred_element_type=jnp.float32)
            * score_scale
        )
        weights = jnp.where(keep, jnp.exp(scores - row_bound.T[:, :, None]), 0.0)
        summed = summed + jnp.sum(weights, axis=2)
        weighted = weighted + jnp.einsum(
            "hqk,khd->qhd",
            weights.astype(jnp.bfloat16),
            value_parts,
            preferred_element_type=jnp.float32,
        )
    tile_out = (weighted / summed.T[:, :, None]).astype(jnp.bfloat16).reshape(tile_len, half)
    mine_rows = lax.dynamic_slice_in_dim(tile_out, parity * row_count, row_count, 0)
    their_rows = lax.dynamic_slice_in_dim(tile_out, (1 - parity) * row_count, row_count, 0)
    back = lax.ppermute(their_rows, seq, partner)
    attended = jnp.where(
        parity == 0,
        jnp.concatenate([mine_rows, back], axis=1),
        jnp.concatenate([back, mine_rows], axis=1),
    )
    spread = jnp.broadcast_to(attended[None], (x_count,) + attended.shape)
    token_parts = lax.all_to_all(spread, "sx", 0, 0)
    terms = jnp.stack(
        [
            jnp.dot(token_parts[j], weight_block, preferred_element_type=jnp.float32).astype(
                jnp.bfloat16
            )
            for j in range(x_count)
        ]
    )
    group_index = lax.axis_index("head")
    mixed = lax.dynamic_index_in_dim(terms, group_index, 0, keepdims=False).astype(jnp.float32)
    for shift in range(1, head_groups):
        outgoing = lax.dynamic_index_in_dim(
            terms, (group_index + shift) % head_groups, 0, keepdims=False
        )
        route = [(g, (g + shift) % head_groups) for g in range(head_groups)]
        mixed = mixed + lax.ppermute(outgoing, "head", route).astype(jnp.float32)
    updated = (stream_block.astype(jnp.float32) + gate_block[None, :] * mixed).astype(jnp.bfloat16)
    hand = linear_pairs(
        (sections, x_count, head_groups), lambda s, a, b: ((s + 1) % sections, b, a)
    )
    handed = lax.ppermute(updated, ("section", "sx", "head"), hand)
    return handed[None]


def solution(mesh):
    sections, seq_count, head_count = mesh.devices.shape
    x_count = 4 if seq_count % 4 == 0 else 1
    split_mesh = Mesh(
        mesh.devices.reshape(sections, x_count, seq_count // x_count, head_count),
        ("section", "sx", "sy", "head"),
    )
    seq = ("sx", "sy")
    in_specs = (
        P("section", seq, "head"),
        P("section", seq, "head"),
        P("section", seq, "head"),
        P("section", seq, "head"),
        P("section", "head", seq),
        P("section", "head"),
        P(),
    )
    out_specs = P("section", seq, "head")
    return jax.shard_map(
        on_device, mesh=split_mesh, in_specs=in_specs, out_specs=out_specs, check_vma=False
    )
```

```python
from functools import partial
import math

import jax
import jax.numpy as jnp
from jax import lax
from jax.sharding import Mesh, PartitionSpec as P

HD = 128
SPATIAL = 1


def shifted(block, axis, count, distance, wanted):
    devices = range(count)
    route = [(i - distance, i) for i in devices if i - distance in devices and wanted(i)]
    return lax.ppermute(block, axis, route)


def needs(offset):
    if offset == 3:
        return lambda i: i % 2 == 1
    if offset == -3:
        return lambda i: i % 2 == 0
    return lambda i: True


def linear_pairs(sizes, mapping):
    def flat(index):
        value = 0
        for part, size in zip(index, sizes):
            value = value * size + part
        return value

    grid = [[]]
    for size in sizes:
        grid = [index + [part] for index in grid for part in range(size)]
    return [(flat(index), flat(mapping(*index))) for index in grid]


def from_behind(value, axis, steps):
    count = lax.axis_size(axis)
    pairs = [(source, (source + steps) % count) for source in range(count)]
    return lax.ppermute(value, axis, pairs)


def split_heads(slab, head_count):
    return slab.reshape(slab.shape[0], head_count, slab.shape[1] // head_count)


def tile_maxima(key_slab, head_count, spatial_count):
    parts = split_heads(key_slab, head_count).astype(jnp.float32)
    lengths = jnp.sqrt(jnp.sum(parts * parts, axis=2))
    return jnp.max(lengths.reshape(spatial_count, -1, head_count), axis=1)


def slab_keep(nearby, slab_tile, in_range, spatial_count, temporal_count):
    first = jnp.clip(slab_tile, 0, temporal_count - 1) * spatial_count
    return lax.dynamic_slice_in_dim(nearby, first, spatial_count, 1) & in_range


def attend(
    running,
    slab_entry,
    keep,
    query_parts,
    row_bound,
    head_count,
    spatial_count,
    tile_rows,
    score_scale,
):
    weighted, summed = running
    row_count = query_parts.shape[0]
    slab_keys = split_heads(slab_entry[0], head_count)
    slab_values = split_heads(slab_entry[1], head_count)
    scores = (
        jnp.einsum("qhd,khd->hqk", query_parts, slab_keys, preferred_element_type=jnp.float32)
        * score_scale
    )
    row_keep = jnp.broadcast_to(
        keep[:, None, :, None], (spatial_count, tile_rows, spatial_count, tile_rows)
    )
    row_keep = row_keep.reshape(row_count, row_count)
    weights = jnp.where(row_keep[None], jnp.exp(scores - row_bound.T[:, :, None]), 0.0)
    summed = summed + jnp.sum(weights, axis=2)
    weighted = weighted + jnp.einsum(
        "hqk,khd->qhd",
        weights.astype(jnp.bfloat16),
        slab_values,
        preferred_element_type=jnp.float32,
    )
    return (weighted, summed)


def on_device(query_heads, key_heads, value_heads, stream, out_weight, gate_scale, windows):
    queries = query_heads[0]
    own_keys = key_heads[0]
    own_values = value_heads[0]
    row_count, feature_count = queries.shape
    head_count = feature_count // HD
    spatial_count = SPATIAL
    tile_rows = row_count // spatial_count
    tile_count = windows.shape[0]
    temporal_count = tile_count // spatial_count
    score_scale = 1.0 / math.sqrt(HD)
    x_count = lax.axis_size("sx")
    y_count = lax.axis_size("sy")
    head_groups = lax.axis_size("head")
    sections = lax.axis_size("section")
    seq_count = x_count * y_count
    x_index = lax.axis_index("sx")
    y_index = lax.axis_index("sy")
    position = x_index * y_count + y_index
    parity = position % 2
    temporal = position // 2
    allowed = jnp.any(
        windows[:, :, None] == jnp.arange(tile_count, dtype=jnp.int32)[None, None, :], axis=1
    )
    row_allowed = lax.dynamic_index_in_dim(allowed, temporal, 0, keepdims=False)
    seq = ("sx", "sy")
    half = feature_count // 2
    own_heads = head_count // 2
    tile_len = 2 * row_count
    partner = [(i, i ^ 1) for i in range(seq_count)]

    def partner_half(block):
        return lax.dynamic_slice_in_dim(block, (1 - parity) * half, half, 1)

    def own_half(block):
        return lax.dynamic_slice_in_dim(block, parity * half, half, 1)

    sent = lax.ppermute(
        (partner_half(queries), partner_half(own_keys), partner_half(own_values)), seq, partner
    )

    def whole_tile(mine, theirs):
        return jnp.where(
            parity == 0,
            jnp.concatenate([mine, theirs], axis=0),
            jnp.concatenate([theirs, mine], axis=0),
        )

    tile_q = whole_tile(own_half(queries), sent[0])
    tile_k = whole_tile(own_half(own_keys), sent[1])
    tile_v = whole_tile(own_half(own_values), sent[2])
    before = lax.ppermute((tile_k, tile_v), seq, [(i, i + 2) for i in range(seq_count - 2)])
    after = lax.ppermute((tile_k, tile_v), seq, [(i, i - 2) for i in range(2, seq_count)])
    key_tiles = [before, (tile_k, tile_v), after]
    keeps = []
    for step in (-1, 0, 1):
        near = temporal + step
        in_range = (near >= 0) & (near < temporal_count)
        listed = lax.dynamic_index_in_dim(
            row_allowed, jnp.clip(near, 0, temporal_count - 1), 0, keepdims=False
        )
        keeps.append(in_range & listed)
    bound = jnp.zeros((own_heads,), jnp.float32)
    for (keys, _), keep in zip(key_tiles, keeps):
        key_float = keys.reshape(tile_len, own_heads, HD).astype(jnp.float32)
        key_lengths = jnp.sqrt(jnp.sum(key_float * key_float, axis=2))
        bound = jnp.maximum(bound, jnp.where(keep, jnp.max(key_lengths, axis=0), 0.0))
    query_parts = tile_q.reshape(tile_len, own_heads, HD)
    query_float = query_parts.astype(jnp.float32)
    query_lengths = jnp.sqrt(jnp.sum(query_float * query_float, axis=2))
    row_bound = query_lengths * bound[None, :] * score_scale
    weight_block = lax.all_gather(out_weight[0], "sy", axis=1, tiled=True)
    swap = linear_pairs((x_count, head_groups), lambda a, b: (b, a))
    stream_in, gate_in, _ = lax.optimization_barrier((stream[0], gate_scale[0], tile_k))
    stream_block = lax.ppermute(stream_in, ("sx", "head"), swap)
    gate_block = lax.ppermute(gate_in, ("sx", "head"), swap)
    weight_block, row_bound, stream_block, gate_block = lax.optimization_barrier(
        (weight_block, row_bound, stream_block, gate_block)
    )
    weighted = jnp.zeros((tile_len, own_heads, HD), jnp.float32)
    summed = jnp.zeros((own_heads, tile_len), jnp.float32)
    for (keys, values), keep in zip(key_tiles, keeps):
        key_parts = keys.reshape(tile_len, own_heads, HD)
        value_parts = values.reshape(tile_len, own_heads, HD)
        scores = (
            jnp.einsum("qhd,khd->hqk", query_parts, key_parts, preferred_element_type=jnp.float32)
            * score_scale
        )
        weights = jnp.where(keep, jnp.exp(scores - row_bound.T[:, :, None]), 0.0)
        summed = summed + jnp.sum(weights, axis=2)
        weighted = weighted + jnp.einsum(
            "hqk,khd->qhd",
            weights.astype(jnp.bfloat16),
            value_parts,
            preferred_element_type=jnp.float32,
        )
    tile_out = (weighted / summed.T[:, :, None]).astype(jnp.bfloat16).reshape(tile_len, half)
    mine_rows = lax.dynamic_slice_in_dim(tile_out, parity * row_count, row_count, 0)
    their_rows = lax.dynamic_slice_in_dim(tile_out, (1 - parity) * row_count, row_count, 0)
    back = lax.ppermute(their_rows, seq, partner)
    attended = jnp.where(
        parity == 0,
        jnp.concatenate([mine_rows, back], axis=1),
        jnp.concatenate([back, mine_rows], axis=1),
    )
    spread = jnp.broadcast_to(attended[None], (x_count,) + attended.shape)
    token_parts = lax.all_to_all(spread, "sx", 0, 0)
    terms = jnp.stack(
        [
            jnp.dot(token_parts[j], weight_block, preferred_element_type=jnp.float32).astype(
                jnp.bfloat16
            )
            for j in range(x_count)
        ]
    )
    group_index = lax.axis_index("head")
    mixed = lax.dynamic_index_in_dim(terms, group_index, 0, keepdims=False).astype(jnp.float32)
    for shift in range(1, head_groups):
        outgoing = lax.dynamic_index_in_dim(
            terms, (group_index + shift) % head_groups, 0, keepdims=False
        )
        route = [(g, (g + shift) % head_groups) for g in range(head_groups)]
        mixed = mixed + lax.ppermute(outgoing, "head", route).astype(jnp.float32)
    updated = (stream_block.astype(jnp.float32) + gate_block[None, :] * mixed).astype(jnp.bfloat16)
    hand = linear_pairs(
        (sections, x_count, head_groups), lambda s, a, b: ((s + 1) % sections, b, a)
    )
    pieces = 4
    step = row_count // pieces
    handed = jnp.concatenate(
        [
            lax.ppermute(updated[k * step:(k + 1) * step], ("section", "sx", "head"), hand)
            for k in range(pieces)
        ],
        axis=0,
    )
    return handed[None]


def solution(mesh):
    sections, seq_count, head_count = mesh.devices.shape
    x_count = 4 if seq_count % 4 == 0 else 1
    split_mesh = Mesh(
        mesh.devices.reshape(sections, x_count, seq_count // x_count, head_count),
        ("section", "sx", "sy", "head"),
    )
    seq = ("sx", "sy")
    in_specs = (
        P("section", seq, "head"),
        P("section", seq, "head"),
        P("section", seq, "head"),
        P("section", seq, "head"),
        P("section", "head", seq),
        P("section", "head"),
        P(),
    )
    out_specs = P("section", seq, "head")
    return jax.shard_map(
        on_device, mesh=split_mesh, in_specs=in_specs, out_specs=out_specs, check_vma=False
    )
```

```python
from functools import partial
import math

import jax
import jax.numpy as jnp
from jax import lax
from jax.sharding import Mesh, PartitionSpec as P

HD = 128
SPATIAL = 1


def shifted(block, axis, count, distance, wanted):
    devices = range(count)
    route = [(i - distance, i) for i in devices if i - distance in devices and wanted(i)]
    return lax.ppermute(block, axis, route)


def needs(offset):
    if offset == 3:
        return lambda i: i % 2 == 1
    if offset == -3:
        return lambda i: i % 2 == 0
    return lambda i: True


def linear_pairs(sizes, mapping):
    def flat(index):
        value = 0
        for part, size in zip(index, sizes):
            value = value * size + part
        return value

    grid = [[]]
    for size in sizes:
        grid = [index + [part] for index in grid for part in range(size)]
    return [(flat(index), flat(mapping(*index))) for index in grid]


def from_behind(value, axis, steps):
    count = lax.axis_size(axis)
    pairs = [(source, (source + steps) % count) for source in range(count)]
    return lax.ppermute(value, axis, pairs)


def split_heads(slab, head_count):
    return slab.reshape(slab.shape[0], head_count, slab.shape[1] // head_count)


def tile_maxima(key_slab, head_count, spatial_count):
    parts = split_heads(key_slab, head_count).astype(jnp.float32)
    lengths = jnp.sqrt(jnp.sum(parts * parts, axis=2))
    return jnp.max(lengths.reshape(spatial_count, -1, head_count), axis=1)


def slab_keep(nearby, slab_tile, in_range, spatial_count, temporal_count):
    first = jnp.clip(slab_tile, 0, temporal_count - 1) * spatial_count
    return lax.dynamic_slice_in_dim(nearby, first, spatial_count, 1) & in_range


def attend(
    running,
    slab_entry,
    keep,
    query_parts,
    row_bound,
    head_count,
    spatial_count,
    tile_rows,
    score_scale,
):
    weighted, summed = running
    row_count = query_parts.shape[0]
    slab_keys = split_heads(slab_entry[0], head_count)
    slab_values = split_heads(slab_entry[1], head_count)
    scores = (
        jnp.einsum("qhd,khd->hqk", query_parts, slab_keys, preferred_element_type=jnp.float32)
        * score_scale
    )
    row_keep = jnp.broadcast_to(
        keep[:, None, :, None], (spatial_count, tile_rows, spatial_count, tile_rows)
    )
    row_keep = row_keep.reshape(row_count, row_count)
    weights = jnp.where(row_keep[None], jnp.exp(scores - row_bound.T[:, :, None]), 0.0)
    summed = summed + jnp.sum(weights, axis=2)
    weighted = weighted + jnp.einsum(
        "hqk,khd->qhd",
        weights.astype(jnp.bfloat16),
        slab_values,
        preferred_element_type=jnp.float32,
    )
    return (weighted, summed)


def on_device(query_heads, key_heads, value_heads, stream, out_weight, gate_scale, windows):
    queries = query_heads[0]
    own_keys = key_heads[0]
    own_values = value_heads[0]
    row_count, feature_count = queries.shape
    head_count = feature_count // HD
    spatial_count = SPATIAL
    tile_rows = row_count // spatial_count
    tile_count = windows.shape[0]
    temporal_count = tile_count // spatial_count
    score_scale = 1.0 / math.sqrt(HD)
    x_count = lax.axis_size("sx")
    y_count = lax.axis_size("sy")
    head_groups = lax.axis_size("head")
    sections = lax.axis_size("section")
    seq_count = x_count * y_count
    x_index = lax.axis_index("sx")
    y_index = lax.axis_index("sy")
    position = x_index * y_count + y_index
    parity = position % 2
    temporal = position // 2
    allowed = jnp.any(
        windows[:, :, None] == jnp.arange(tile_count, dtype=jnp.int32)[None, None, :], axis=1
    )
    row_allowed = lax.dynamic_index_in_dim(allowed, temporal, 0, keepdims=False)
    seq = ("sx", "sy")
    half = feature_count // 2
    own_heads = head_count // 2
    tile_len = 2 * row_count
    partner = [(i, i ^ 1) for i in range(seq_count)]

    def partner_half(block):
        return lax.dynamic_slice_in_dim(block, (1 - parity) * half, half, 1)

    def own_half(block):
        return lax.dynamic_slice_in_dim(block, parity * half, half, 1)

    sent = lax.ppermute(
        (partner_half(queries), partner_half(own_keys), partner_half(own_values)), seq, partner
    )

    def whole_tile(mine, theirs):
        return jnp.where(
            parity == 0,
            jnp.concatenate([mine, theirs], axis=0),
            jnp.concatenate([theirs, mine], axis=0),
        )

    tile_q = whole_tile(own_half(queries), sent[0])
    tile_k = whole_tile(own_half(own_keys), sent[1])
    tile_v = whole_tile(own_half(own_values), sent[2])
    before = lax.ppermute((tile_k, tile_v), seq, [(i, i + 2) for i in range(seq_count - 2)])
    after = lax.ppermute((tile_k, tile_v), seq, [(i, i - 2) for i in range(2, seq_count)])
    key_tiles = [before, (tile_k, tile_v), after]
    keeps = []
    for step in (-1, 0, 1):
        near = temporal + step
        in_range = (near >= 0) & (near < temporal_count)
        listed = lax.dynamic_index_in_dim(
            row_allowed, jnp.clip(near, 0, temporal_count - 1), 0, keepdims=False
        )
        keeps.append(in_range & listed)
    bound = jnp.zeros((own_heads,), jnp.float32)
    for (keys, _), keep in zip(key_tiles, keeps):
        key_float = keys.reshape(tile_len, own_heads, HD).astype(jnp.float32)
        key_lengths = jnp.sqrt(jnp.sum(key_float * key_float, axis=2))
        bound = jnp.maximum(bound, jnp.where(keep, jnp.max(key_lengths, axis=0), 0.0))
    query_parts = tile_q.reshape(tile_len, own_heads, HD)
    query_float = query_parts.astype(jnp.float32)
    query_lengths = jnp.sqrt(jnp.sum(query_float * query_float, axis=2))
    row_bound = query_lengths * bound[None, :] * score_scale
    weight_block = lax.all_gather(out_weight[0], "sy", axis=1, tiled=True)
    swap = linear_pairs((x_count, head_groups), lambda a, b: (b, a))
    stream_in, gate_in, _ = lax.optimization_barrier((stream[0], gate_scale[0], tile_k))
    stream_block = lax.ppermute(stream_in, ("sx", "head"), swap)
    gate_block = lax.ppermute(gate_in, ("sx", "head"), swap)
    weight_block, row_bound, stream_block, gate_block = lax.optimization_barrier(
        (weight_block, row_bound, stream_block, gate_block)
    )
    def attend_rows(first):
        rows_q = lax.dynamic_slice_in_dim(query_parts, first, row_count, 0)
        rows_bound = lax.dynamic_slice_in_dim(row_bound, first, row_count, 0)
        weighted = jnp.zeros((row_count, own_heads, HD), jnp.float32)
        summed = jnp.zeros((own_heads, row_count), jnp.float32)
        for (keys, values), keep in zip(key_tiles, keeps):
            key_parts = keys.reshape(tile_len, own_heads, HD)
            value_parts = values.reshape(tile_len, own_heads, HD)
            scores = (
                jnp.einsum(
                    "qhd,khd->hqk", rows_q, key_parts, preferred_element_type=jnp.float32
                )
                * score_scale
            )
            weights = jnp.where(keep, jnp.exp(scores - rows_bound.T[:, :, None]), 0.0)
            summed = summed + jnp.sum(weights, axis=2)
            weighted = weighted + jnp.einsum(
                "hqk,khd->qhd",
                weights.astype(jnp.bfloat16),
                value_parts,
                preferred_element_type=jnp.float32,
            )
        return (weighted / summed.T[:, :, None]).astype(jnp.bfloat16).reshape(row_count, half)

    their_rows = attend_rows((1 - parity) * row_count)
    back = lax.ppermute(their_rows, seq, partner)
    mine_rows = attend_rows(parity * row_count)
    attended = jnp.where(
        parity == 0,
        jnp.concatenate([mine_rows, back], axis=1),
        jnp.concatenate([back, mine_rows], axis=1),
    )
    spread = jnp.broadcast_to(attended[None], (x_count,) + attended.shape)
    token_parts = lax.all_to_all(spread, "sx", 0, 0)
    terms = jnp.stack(
        [
            jnp.dot(token_parts[j], weight_block, preferred_element_type=jnp.float32).astype(
                jnp.bfloat16
            )
            for j in range(x_count)
        ]
    )
    group_index = lax.axis_index("head")
    mixed = lax.dynamic_index_in_dim(terms, group_index, 0, keepdims=False).astype(jnp.float32)
    for shift in range(1, head_groups):
        outgoing = lax.dynamic_index_in_dim(
            terms, (group_index + shift) % head_groups, 0, keepdims=False
        )
        route = [(g, (g + shift) % head_groups) for g in range(head_groups)]
        mixed = mixed + lax.ppermute(outgoing, "head", route).astype(jnp.float32)
    updated = (stream_block.astype(jnp.float32) + gate_block[None, :] * mixed).astype(jnp.bfloat16)
    hand = linear_pairs(
        (sections, x_count, head_groups), lambda s, a, b: ((s + 1) % sections, b, a)
    )
    handed = lax.ppermute(updated, ("section", "sx", "head"), hand)
    return handed[None]


def solution(mesh):
    sections, seq_count, head_count = mesh.devices.shape
    x_count = 4 if seq_count % 4 == 0 else 1
    split_mesh = Mesh(
        mesh.devices.reshape(sections, x_count, seq_count // x_count, head_count),
        ("section", "sx", "sy", "head"),
    )
    seq = ("sx", "sy")
    in_specs = (
        P("section", seq, "head"),
        P("section", seq, "head"),
        P("section", seq, "head"),
        P("section", seq, "head"),
        P("section", "head", seq),
        P("section", "head"),
        P(),
    )
    out_specs = P("section", seq, "head")
    return jax.shard_map(
        on_device, mesh=split_mesh, in_specs=in_specs, out_specs=out_specs, check_vma=False
    )
```

```python
from functools import partial
import math

import jax
import jax.numpy as jnp
from jax import lax
from jax.sharding import Mesh, PartitionSpec as P

HD = 128
SPATIAL = 1


def shifted(block, axis, count, distance, wanted):
    devices = range(count)
    route = [(i - distance, i) for i in devices if i - distance in devices and wanted(i)]
    return lax.ppermute(block, axis, route)


def needs(offset):
    if offset == 3:
        return lambda i: i % 2 == 1
    if offset == -3:
        return lambda i: i % 2 == 0
    return lambda i: True


def linear_pairs(sizes, mapping):
    def flat(index):
        value = 0
        for part, size in zip(index, sizes):
            value = value * size + part
        return value

    grid = [[]]
    for size in sizes:
        grid = [index + [part] for index in grid for part in range(size)]
    return [(flat(index), flat(mapping(*index))) for index in grid]


def from_behind(value, axis, steps):
    count = lax.axis_size(axis)
    pairs = [(source, (source + steps) % count) for source in range(count)]
    return lax.ppermute(value, axis, pairs)


def split_heads(slab, head_count):
    return slab.reshape(slab.shape[0], head_count, slab.shape[1] // head_count)


def tile_maxima(key_slab, head_count, spatial_count):
    parts = split_heads(key_slab, head_count).astype(jnp.float32)
    lengths = jnp.sqrt(jnp.sum(parts * parts, axis=2))
    return jnp.max(lengths.reshape(spatial_count, -1, head_count), axis=1)


def slab_keep(nearby, slab_tile, in_range, spatial_count, temporal_count):
    first = jnp.clip(slab_tile, 0, temporal_count - 1) * spatial_count
    return lax.dynamic_slice_in_dim(nearby, first, spatial_count, 1) & in_range


def attend(
    running,
    slab_entry,
    keep,
    query_parts,
    row_bound,
    head_count,
    spatial_count,
    tile_rows,
    score_scale,
):
    weighted, summed = running
    row_count = query_parts.shape[0]
    slab_keys = split_heads(slab_entry[0], head_count)
    slab_values = split_heads(slab_entry[1], head_count)
    scores = (
        jnp.einsum("qhd,khd->hqk", query_parts, slab_keys, preferred_element_type=jnp.float32)
        * score_scale
    )
    row_keep = jnp.broadcast_to(
        keep[:, None, :, None], (spatial_count, tile_rows, spatial_count, tile_rows)
    )
    row_keep = row_keep.reshape(row_count, row_count)
    weights = jnp.where(row_keep[None], jnp.exp(scores - row_bound.T[:, :, None]), 0.0)
    summed = summed + jnp.sum(weights, axis=2)
    weighted = weighted + jnp.einsum(
        "hqk,khd->qhd",
        weights.astype(jnp.bfloat16),
        slab_values,
        preferred_element_type=jnp.float32,
    )
    return (weighted, summed)


def on_device(query_heads, key_heads, value_heads, stream, out_weight, gate_scale, windows):
    queries = query_heads[0]
    own_keys = key_heads[0]
    own_values = value_heads[0]
    row_count, feature_count = queries.shape
    head_count = feature_count // HD
    spatial_count = SPATIAL
    tile_rows = row_count // spatial_count
    tile_count = windows.shape[0]
    temporal_count = tile_count // spatial_count
    score_scale = 1.0 / math.sqrt(HD)
    x_count = lax.axis_size("sx")
    y_count = lax.axis_size("sy")
    head_groups = lax.axis_size("head")
    sections = lax.axis_size("section")
    seq_count = x_count * y_count
    x_index = lax.axis_index("sx")
    y_index = lax.axis_index("sy")
    position = x_index * y_count + y_index
    parity = position % 2
    temporal = position // 2
    allowed = jnp.any(
        windows[:, :, None] == jnp.arange(tile_count, dtype=jnp.int32)[None, None, :], axis=1
    )
    row_allowed = lax.dynamic_index_in_dim(allowed, temporal, 0, keepdims=False)
    seq = ("sx", "sy")
    half = feature_count // 2
    own_heads = head_count // 2
    tile_len = 2 * row_count
    partner = [(i, i ^ 1) for i in range(seq_count)]

    def partner_half(block):
        return lax.dynamic_slice_in_dim(block, (1 - parity) * half, half, 1)

    def own_half(block):
        return lax.dynamic_slice_in_dim(block, parity * half, half, 1)

    sent = lax.ppermute(
        (partner_half(queries), partner_half(own_keys), partner_half(own_values)), seq, partner
    )

    def whole_tile(mine, theirs):
        return jnp.where(
            parity == 0,
            jnp.concatenate([mine, theirs], axis=0),
            jnp.concatenate([theirs, mine], axis=0),
        )

    tile_q = whole_tile(own_half(queries), sent[0])
    tile_k = whole_tile(own_half(own_keys), sent[1])
    tile_v = whole_tile(own_half(own_values), sent[2])
    before = lax.ppermute((tile_k, tile_v), seq, [(i, i + 2) for i in range(seq_count - 2)])
    after = lax.ppermute((tile_k, tile_v), seq, [(i, i - 2) for i in range(2, seq_count)])
    key_tiles = [before, (tile_k, tile_v), after]
    keeps = []
    for step in (-1, 0, 1):
        near = temporal + step
        in_range = (near >= 0) & (near < temporal_count)
        listed = lax.dynamic_index_in_dim(
            row_allowed, jnp.clip(near, 0, temporal_count - 1), 0, keepdims=False
        )
        keeps.append(in_range & listed)
    bound = jnp.zeros((own_heads,), jnp.float32)
    for (keys, _), keep in zip(key_tiles, keeps):
        key_float = keys.reshape(tile_len, own_heads, HD).astype(jnp.float32)
        key_lengths = jnp.sqrt(jnp.sum(key_float * key_float, axis=2))
        bound = jnp.maximum(bound, jnp.where(keep, jnp.max(key_lengths, axis=0), 0.0))
    query_parts = tile_q.reshape(tile_len, own_heads, HD)
    query_float = query_parts.astype(jnp.float32)
    query_lengths = jnp.sqrt(jnp.sum(query_float * query_float, axis=2))
    row_bound = query_lengths * bound[None, :] * score_scale
    weight_block = lax.all_gather(out_weight[0], "sy", axis=1, tiled=True)
    swap = linear_pairs((x_count, head_groups), lambda a, b: (b, a))
    stream_in, gate_in, _ = lax.optimization_barrier((stream[0], gate_scale[0], tile_k))
    stream_block = lax.ppermute(stream_in, ("sx", "head"), swap)
    gate_block = lax.ppermute(gate_in, ("sx", "head"), swap)
    row_bound, stream_block, gate_block = lax.optimization_barrier(
        (row_bound, stream_block, gate_block)
    )
    weighted = jnp.zeros((tile_len, own_heads, HD), jnp.float32)
    summed = jnp.zeros((own_heads, tile_len), jnp.float32)
    for (keys, values), keep in zip(key_tiles, keeps):
        key_parts = keys.reshape(tile_len, own_heads, HD)
        value_parts = values.reshape(tile_len, own_heads, HD)
        scores = (
            jnp.einsum("qhd,khd->hqk", query_parts, key_parts, preferred_element_type=jnp.float32)
            * score_scale
        )
        weights = jnp.where(keep, jnp.exp(scores - row_bound.T[:, :, None]), 0.0)
        summed = summed + jnp.sum(weights, axis=2)
        weighted = weighted + jnp.einsum(
            "hqk,khd->qhd",
            weights.astype(jnp.bfloat16),
            value_parts,
            preferred_element_type=jnp.float32,
        )
    tile_out = (weighted / summed.T[:, :, None]).astype(jnp.bfloat16).reshape(tile_len, half)
    mine_rows = lax.dynamic_slice_in_dim(tile_out, parity * row_count, row_count, 0)
    their_rows = lax.dynamic_slice_in_dim(tile_out, (1 - parity) * row_count, row_count, 0)
    back = lax.ppermute(their_rows, seq, partner)
    attended = jnp.where(
        parity == 0,
        jnp.concatenate([mine_rows, back], axis=1),
        jnp.concatenate([back, mine_rows], axis=1),
    )
    weight_block, attended = lax.optimization_barrier((weight_block, attended))
    spread = jnp.broadcast_to(attended[None], (x_count,) + attended.shape)
    token_parts = lax.all_to_all(spread, "sx", 0, 0)
    terms = jnp.stack(
        [
            jnp.dot(token_parts[j], weight_block, preferred_element_type=jnp.float32).astype(
                jnp.bfloat16
            )
            for j in range(x_count)
        ]
    )
    group_index = lax.axis_index("head")
    mixed = lax.dynamic_index_in_dim(terms, group_index, 0, keepdims=False).astype(jnp.float32)
    for shift in range(1, head_groups):
        outgoing = lax.dynamic_index_in_dim(
            terms, (group_index + shift) % head_groups, 0, keepdims=False
        )
        route = [(g, (g + shift) % head_groups) for g in range(head_groups)]
        mixed = mixed + lax.ppermute(outgoing, "head", route).astype(jnp.float32)
    updated = (stream_block.astype(jnp.float32) + gate_block[None, :] * mixed).astype(jnp.bfloat16)
    hand = linear_pairs(
        (sections, x_count, head_groups), lambda s, a, b: ((s + 1) % sections, b, a)
    )
    handed = lax.ppermute(updated, ("section", "sx", "head"), hand)
    return handed[None]


def solution(mesh):
    sections, seq_count, head_count = mesh.devices.shape
    x_count = 4 if seq_count % 4 == 0 else 1
    split_mesh = Mesh(
        mesh.devices.reshape(sections, x_count, seq_count // x_count, head_count),
        ("section", "sx", "sy", "head"),
    )
    seq = ("sx", "sy")
    in_specs = (
        P("section", seq, "head"),
        P("section", seq, "head"),
        P("section", seq, "head"),
        P("section", seq, "head"),
        P("section", "head", seq),
        P("section", "head"),
        P(),
    )
    out_specs = P("section", seq, "head")
    return jax.shard_map(
        on_device, mesh=split_mesh, in_specs=in_specs, out_specs=out_specs, check_vma=False
    )
```

```python
from functools import partial
import math

import jax
import jax.numpy as jnp
from jax import lax
from jax.sharding import Mesh, PartitionSpec as P

HD = 128
SPATIAL = 1


def shifted(block, axis, count, distance, wanted):
    devices = range(count)
    route = [(i - distance, i) for i in devices if i - distance in devices and wanted(i)]
    return lax.ppermute(block, axis, route)


def needs(offset):
    if offset == 3:
        return lambda i: i % 2 == 1
    if offset == -3:
        return lambda i: i % 2 == 0
    return lambda i: True


def linear_pairs(sizes, mapping):
    def flat(index):
        value = 0
        for part, size in zip(index, sizes):
            value = value * size + part
        return value

    grid = [[]]
    for size in sizes:
        grid = [index + [part] for index in grid for part in range(size)]
    return [(flat(index), flat(mapping(*index))) for index in grid]


def from_behind(value, axis, steps):
    count = lax.axis_size(axis)
    pairs = [(source, (source + steps) % count) for source in range(count)]
    return lax.ppermute(value, axis, pairs)


def split_heads(slab, head_count):
    return slab.reshape(slab.shape[0], head_count, slab.shape[1] // head_count)


def tile_maxima(key_slab, head_count, spatial_count):
    parts = split_heads(key_slab, head_count).astype(jnp.float32)
    lengths = jnp.sqrt(jnp.sum(parts * parts, axis=2))
    return jnp.max(lengths.reshape(spatial_count, -1, head_count), axis=1)


def slab_keep(nearby, slab_tile, in_range, spatial_count, temporal_count):
    first = jnp.clip(slab_tile, 0, temporal_count - 1) * spatial_count
    return lax.dynamic_slice_in_dim(nearby, first, spatial_count, 1) & in_range


def attend(
    running,
    slab_entry,
    keep,
    query_parts,
    row_bound,
    head_count,
    spatial_count,
    tile_rows,
    score_scale,
):
    weighted, summed = running
    row_count = query_parts.shape[0]
    slab_keys = split_heads(slab_entry[0], head_count)
    slab_values = split_heads(slab_entry[1], head_count)
    scores = (
        jnp.einsum("qhd,khd->hqk", query_parts, slab_keys, preferred_element_type=jnp.float32)
        * score_scale
    )
    row_keep = jnp.broadcast_to(
        keep[:, None, :, None], (spatial_count, tile_rows, spatial_count, tile_rows)
    )
    row_keep = row_keep.reshape(row_count, row_count)
    weights = jnp.where(row_keep[None], jnp.exp(scores - row_bound.T[:, :, None]), 0.0)
    summed = summed + jnp.sum(weights, axis=2)
    weighted = weighted + jnp.einsum(
        "hqk,khd->qhd",
        weights.astype(jnp.bfloat16),
        slab_values,
        preferred_element_type=jnp.float32,
    )
    return (weighted, summed)


def on_device(query_heads, key_heads, value_heads, stream, out_weight, gate_scale, windows):
    queries = query_heads[0]
    own_keys = key_heads[0]
    own_values = value_heads[0]
    row_count, feature_count = queries.shape
    head_count = feature_count // HD
    spatial_count = SPATIAL
    tile_rows = row_count // spatial_count
    tile_count = windows.shape[0]
    temporal_count = tile_count // spatial_count
    score_scale = 1.0 / math.sqrt(HD)
    x_count = lax.axis_size("sx")
    y_count = lax.axis_size("sy")
    head_groups = lax.axis_size("head")
    sections = lax.axis_size("section")
    seq_count = x_count * y_count
    x_index = lax.axis_index("sx")
    y_index = lax.axis_index("sy")
    position = x_index * y_count + y_index
    parity = position % 2
    temporal = position // 2
    allowed = jnp.any(
        windows[:, :, None] == jnp.arange(tile_count, dtype=jnp.int32)[None, None, :], axis=1
    )
    row_allowed = lax.dynamic_index_in_dim(allowed, temporal, 0, keepdims=False)
    seq = ("sx", "sy")
    half = feature_count // 2
    own_heads = head_count // 2
    tile_len = 2 * row_count
    partner = [(i, i ^ 1) for i in range(seq_count)]

    def partner_half(block):
        return lax.dynamic_slice_in_dim(block, (1 - parity) * half, half, 1)

    def own_half(block):
        return lax.dynamic_slice_in_dim(block, parity * half, half, 1)

    sent = lax.ppermute(
        (partner_half(queries), partner_half(own_keys), partner_half(own_values)), seq, partner
    )

    def whole_tile(mine, theirs):
        return jnp.where(
            parity == 0,
            jnp.concatenate([mine, theirs], axis=0),
            jnp.concatenate([theirs, mine], axis=0),
        )

    tile_q = whole_tile(own_half(queries), sent[0])
    tile_k = whole_tile(own_half(own_keys), sent[1])
    tile_v = whole_tile(own_half(own_values), sent[2])
    before = lax.ppermute((tile_k, tile_v), seq, [(i, i + 2) for i in range(seq_count - 2)])
    after = lax.ppermute((tile_k, tile_v), seq, [(i, i - 2) for i in range(2, seq_count)])
    key_tiles = [before, (tile_k, tile_v), after]
    keeps = []
    for step in (-1, 0, 1):
        near = temporal + step
        in_range = (near >= 0) & (near < temporal_count)
        listed = lax.dynamic_index_in_dim(
            row_allowed, jnp.clip(near, 0, temporal_count - 1), 0, keepdims=False
        )
        keeps.append(in_range & listed)
    bound = jnp.zeros((own_heads,), jnp.float32)
    for (keys, _), keep in zip(key_tiles, keeps):
        key_float = keys.reshape(tile_len, own_heads, HD).astype(jnp.float32)
        key_lengths = jnp.sqrt(jnp.sum(key_float * key_float, axis=2))
        bound = jnp.maximum(bound, jnp.where(keep, jnp.max(key_lengths, axis=0), 0.0))
    query_parts = tile_q.reshape(tile_len, own_heads, HD)
    query_float = query_parts.astype(jnp.float32)
    query_lengths = jnp.sqrt(jnp.sum(query_float * query_float, axis=2))
    row_bound = query_lengths * bound[None, :] * score_scale
    weight_block = lax.all_gather(out_weight[0], "sy", axis=1, tiled=True)
    swap = linear_pairs((x_count, head_groups), lambda a, b: (b, a))
    stream_in, gate_in, _ = lax.optimization_barrier((stream[0], gate_scale[0], tile_k))
    stream_block = lax.ppermute(stream_in, ("sx", "head"), swap)
    gate_block = lax.ppermute(gate_in, ("sx", "head"), swap)
    weight_block, row_bound, stream_block, gate_block = lax.optimization_barrier(
        (weight_block, row_bound, stream_block, gate_block)
    )
    weighted = jnp.zeros((tile_len, own_heads, HD), jnp.float32)
    summed = jnp.zeros((own_heads, tile_len), jnp.float32)
    for (keys, values), keep in zip(key_tiles, keeps):
        key_parts = keys.reshape(tile_len, own_heads, HD)
        value_parts = values.reshape(tile_len, own_heads, HD)
        scores = (
            jnp.einsum("qhd,khd->hqk", query_parts, key_parts, preferred_element_type=jnp.float32)
            * score_scale
        )
        weights = jnp.where(keep, jnp.exp(scores - row_bound.T[:, :, None]), 0.0)
        summed = summed + jnp.sum(weights, axis=2)
        weighted = weighted + jnp.einsum(
            "hqk,khd->qhd",
            weights.astype(jnp.bfloat16),
            value_parts,
            preferred_element_type=jnp.float32,
        )
    tile_out = (weighted / summed.T[:, :, None]).astype(jnp.bfloat16).reshape(tile_len, half)
    mine_rows = lax.dynamic_slice_in_dim(tile_out, parity * row_count, row_count, 0)
    their_rows = lax.dynamic_slice_in_dim(tile_out, (1 - parity) * row_count, row_count, 0)
    back = lax.ppermute(their_rows, seq, partner)
    attended = jnp.where(
        parity == 0,
        jnp.concatenate([mine_rows, back], axis=1),
        jnp.concatenate([back, mine_rows], axis=1),
    )
    spread = jnp.broadcast_to(attended[None], (x_count,) + attended.shape)
    token_parts = lax.all_to_all(spread, "sx", 0, 0)
    group_index = lax.axis_index("head")

    def term_for(slab_x):
        part = lax.dynamic_index_in_dim(token_parts, slab_x, 0, keepdims=False)
        return jnp.dot(part, weight_block, preferred_element_type=jnp.float32).astype(
            jnp.bfloat16
        )

    received = []
    for shift in range(1, head_groups):
        outgoing = term_for((group_index + shift) % head_groups)
        route = [(g, (g + shift) % head_groups) for g in range(head_groups)]
        received.append(lax.ppermute(outgoing, "head", route))
    mixed = term_for(group_index).astype(jnp.float32)
    for term in received:
        mixed = mixed + term.astype(jnp.float32)
    updated = (stream_block.astype(jnp.float32) + gate_block[None, :] * mixed).astype(jnp.bfloat16)
    hand = linear_pairs(
        (sections, x_count, head_groups), lambda s, a, b: ((s + 1) % sections, b, a)
    )
    handed = lax.ppermute(updated, ("section", "sx", "head"), hand)
    return handed[None]


def solution(mesh):
    sections, seq_count, head_count = mesh.devices.shape
    x_count = 4 if seq_count % 4 == 0 else 1
    split_mesh = Mesh(
        mesh.devices.reshape(sections, x_count, seq_count // x_count, head_count),
        ("section", "sx", "sy", "head"),
    )
    seq = ("sx", "sy")
    in_specs = (
        P("section", seq, "head"),
        P("section", seq, "head"),
        P("section", seq, "head"),
        P("section", seq, "head"),
        P("section", "head", seq),
        P("section", "head"),
        P(),
    )
    out_specs = P("section", seq, "head")
    return jax.shard_map(
        on_device, mesh=split_mesh, in_specs=in_specs, out_specs=out_specs, check_vma=False
    )
```

```python
from functools import partial
import math

import jax
import jax.numpy as jnp
from jax import lax
from jax.sharding import Mesh, PartitionSpec as P

HD = 128
SPATIAL = 1


def shifted(block, axis, count, distance, wanted):
    devices = range(count)
    route = [(i - distance, i) for i in devices if i - distance in devices and wanted(i)]
    return lax.ppermute(block, axis, route)


def needs(offset):
    if offset == 3:
        return lambda i: i % 2 == 1
    if offset == -3:
        return lambda i: i % 2 == 0
    return lambda i: True


def linear_pairs(sizes, mapping):
    def flat(index):
        value = 0
        for part, size in zip(index, sizes):
            value = value * size + part
        return value

    grid = [[]]
    for size in sizes:
        grid = [index + [part] for index in grid for part in range(size)]
    return [(flat(index), flat(mapping(*index))) for index in grid]


def from_behind(value, axis, steps):
    count = lax.axis_size(axis)
    pairs = [(source, (source + steps) % count) for source in range(count)]
    return lax.ppermute(value, axis, pairs)


def split_heads(slab, head_count):
    return slab.reshape(slab.shape[0], head_count, slab.shape[1] // head_count)


def tile_maxima(key_slab, head_count, spatial_count):
    parts = split_heads(key_slab, head_count).astype(jnp.float32)
    lengths = jnp.sqrt(jnp.sum(parts * parts, axis=2))
    return jnp.max(lengths.reshape(spatial_count, -1, head_count), axis=1)


def slab_keep(nearby, slab_tile, in_range, spatial_count, temporal_count):
    first = jnp.clip(slab_tile, 0, temporal_count - 1) * spatial_count
    return lax.dynamic_slice_in_dim(nearby, first, spatial_count, 1) & in_range


def attend(
    running,
    slab_entry,
    keep,
    query_parts,
    row_bound,
    head_count,
    spatial_count,
    tile_rows,
    score_scale,
):
    weighted, summed = running
    row_count = query_parts.shape[0]
    slab_keys = split_heads(slab_entry[0], head_count)
    slab_values = split_heads(slab_entry[1], head_count)
    scores = (
        jnp.einsum("qhd,khd->hqk", query_parts, slab_keys, preferred_element_type=jnp.float32)
        * score_scale
    )
    row_keep = jnp.broadcast_to(
        keep[:, None, :, None], (spatial_count, tile_rows, spatial_count, tile_rows)
    )
    row_keep = row_keep.reshape(row_count, row_count)
    weights = jnp.where(row_keep[None], jnp.exp(scores - row_bound.T[:, :, None]), 0.0)
    summed = summed + jnp.sum(weights, axis=2)
    weighted = weighted + jnp.einsum(
        "hqk,khd->qhd",
        weights.astype(jnp.bfloat16),
        slab_values,
        preferred_element_type=jnp.float32,
    )
    return (weighted, summed)


def on_device(query_heads, key_heads, value_heads, stream, out_weight, gate_scale, windows):
    queries = query_heads[0]
    own_keys = key_heads[0]
    own_values = value_heads[0]
    row_count, feature_count = queries.shape
    head_count = feature_count // HD
    spatial_count = SPATIAL
    tile_rows = row_count // spatial_count
    tile_count = windows.shape[0]
    temporal_count = tile_count // spatial_count
    score_scale = 1.0 / math.sqrt(HD)
    x_count = lax.axis_size("sx")
    y_count = lax.axis_size("sy")
    head_groups = lax.axis_size("head")
    sections = lax.axis_size("section")
    seq_count = x_count * y_count
    x_index = lax.axis_index("sx")
    y_index = lax.axis_index("sy")
    position = x_index * y_count + y_index
    parity = position % 2
    temporal = position // 2
    allowed = jnp.any(
        windows[:, :, None] == jnp.arange(tile_count, dtype=jnp.int32)[None, None, :], axis=1
    )
    row_allowed = lax.dynamic_index_in_dim(allowed, temporal, 0, keepdims=False)
    seq = ("sx", "sy")
    half = feature_count // 2
    own_heads = head_count // 2
    tile_len = 2 * row_count
    partner = [(i, i ^ 1) for i in range(seq_count)]

    def partner_half(block):
        return lax.dynamic_slice_in_dim(block, (1 - parity) * half, half, 1)

    def own_half(block):
        return lax.dynamic_slice_in_dim(block, parity * half, half, 1)

    sent = lax.ppermute(
        (partner_half(queries), partner_half(own_keys), partner_half(own_values)), seq, partner
    )

    def whole_tile(mine, theirs):
        return jnp.where(
            parity == 0,
            jnp.concatenate([mine, theirs], axis=0),
            jnp.concatenate([theirs, mine], axis=0),
        )

    tile_q = whole_tile(own_half(queries), sent[0])
    tile_k = whole_tile(own_half(own_keys), sent[1])
    tile_v = whole_tile(own_half(own_values), sent[2])
    before = lax.ppermute((tile_k, tile_v), seq, [(i, i + 2) for i in range(seq_count - 2)])
    after = lax.ppermute((tile_k, tile_v), seq, [(i, i - 2) for i in range(2, seq_count)])
    key_tiles = [before, (tile_k, tile_v), after]
    keeps = []
    for step in (-1, 0, 1):
        near = temporal + step
        in_range = (near >= 0) & (near < temporal_count)
        listed = lax.dynamic_index_in_dim(
            row_allowed, jnp.clip(near, 0, temporal_count - 1), 0, keepdims=False
        )
        keeps.append(in_range & listed)
    bound = jnp.zeros((own_heads,), jnp.float32)
    for (keys, _), keep in zip(key_tiles, keeps):
        key_float = keys.reshape(tile_len, own_heads, HD).astype(jnp.float32)
        key_lengths = jnp.sqrt(jnp.sum(key_float * key_float, axis=2))
        bound = jnp.maximum(bound, jnp.where(keep, jnp.max(key_lengths, axis=0), 0.0))
    query_parts = tile_q.reshape(tile_len, own_heads, HD)
    query_float = query_parts.astype(jnp.float32)
    query_lengths = jnp.sqrt(jnp.sum(query_float * query_float, axis=2))
    row_bound = query_lengths * bound[None, :] * score_scale
    weight_block = lax.all_gather(out_weight[0], "sy", axis=1, tiled=True)
    swap = linear_pairs((x_count, head_groups), lambda a, b: (b, a))
    stream_in, gate_in, _ = lax.optimization_barrier((stream[0], gate_scale[0], tile_k))
    stream_block = lax.ppermute(stream_in, ("sx", "head"), swap)
    gate_block = lax.ppermute(gate_in, ("sx", "head"), swap)
    weight_block, row_bound, stream_block, gate_block = lax.optimization_barrier(
        (weight_block, row_bound, stream_block, gate_block)
    )
    weighted = jnp.zeros((tile_len, own_heads, HD), jnp.float32)
    summed = jnp.zeros((own_heads, tile_len), jnp.float32)
    for (keys, values), keep in zip(key_tiles, keeps):
        key_parts = keys.reshape(tile_len, own_heads, HD)
        value_parts = values.reshape(tile_len, own_heads, HD)
        scores = (
            jnp.einsum("qhd,khd->hqk", query_parts, key_parts, preferred_element_type=jnp.float32)
            * score_scale
        )
        weights = jnp.where(keep, jnp.exp(scores - row_bound.T[:, :, None]), 0.0)
        summed = summed + jnp.sum(weights, axis=2)
        weighted = weighted + jnp.einsum(
            "hqk,khd->qhd",
            weights.astype(jnp.bfloat16),
            value_parts,
            preferred_element_type=jnp.float32,
        )
    tile_out = (weighted / summed.T[:, :, None]).astype(jnp.bfloat16).reshape(tile_len, half)
    mine_rows = lax.dynamic_slice_in_dim(tile_out, parity * row_count, row_count, 0)
    their_rows = lax.dynamic_slice_in_dim(tile_out, (1 - parity) * row_count, row_count, 0)
    back = lax.ppermute(their_rows, seq, partner)
    attended = jnp.where(
        parity == 0,
        jnp.concatenate([mine_rows, back], axis=1),
        jnp.concatenate([back, mine_rows], axis=1),
    )
    spread = jnp.broadcast_to(attended[None], (x_count,) + attended.shape)
    token_parts = lax.all_to_all(spread, "sx", 0, 0)
    group_index = lax.axis_index("head")

    def term_for(slab_x):
        part = lax.dynamic_index_in_dim(token_parts, slab_x, 0, keepdims=False)
        return jnp.dot(part, weight_block, preferred_element_type=jnp.float32).astype(
            jnp.bfloat16
        )

    received = []
    order = sorted(range(1, head_groups), key=lambda d: -min(d, head_groups - d))
    for shift in order:
        outgoing = term_for((group_index + shift) % head_groups)
        route = [(g, (g + shift) % head_groups) for g in range(head_groups)]
        received.append(lax.ppermute(outgoing, "head", route))
    mixed = term_for(group_index).astype(jnp.float32)
    for term in received:
        mixed = mixed + term.astype(jnp.float32)
    updated = (stream_block.astype(jnp.float32) + gate_block[None, :] * mixed).astype(jnp.bfloat16)
    hand = linear_pairs(
        (sections, x_count, head_groups), lambda s, a, b: ((s + 1) % sections, b, a)
    )
    handed = lax.ppermute(updated, ("section", "sx", "head"), hand)
    return handed[None]


def solution(mesh):
    sections, seq_count, head_count = mesh.devices.shape
    x_count = 4 if seq_count % 4 == 0 else 1
    split_mesh = Mesh(
        mesh.devices.reshape(sections, x_count, seq_count // x_count, head_count),
        ("section", "sx", "sy", "head"),
    )
    seq = ("sx", "sy")
    in_specs = (
        P("section", seq, "head"),
        P("section", seq, "head"),
        P("section", seq, "head"),
        P("section", seq, "head"),
        P("section", "head", seq),
        P("section", "head"),
        P(),
    )
    out_specs = P("section", seq, "head")
    return jax.shard_map(
        on_device, mesh=split_mesh, in_specs=in_specs, out_specs=out_specs, check_vma=False
    )
```
